32 devices in a mesh: dp: 8 (over z, y), mp: 4 (over x, core).
Axes of the slice: x: 2, y: 2, z: 4, core: 2. Of those that a mesh axis runs over, the one named last changes fastest.
Arguments:
- gradients: bfloat16 [8, 4, 192, 16384], P('dp', 'mp'), may hold values from -3000 to 3000
- owner_list: int32 [192], replicated, may hold values from 0 to 7, as said below
- master_weights: float32 [4, 288, 16384], P('mp', 'dp'), may hold values from -6 to 6
- first_moment: float32 [4, 288, 16384], P('mp', 'dp'), may hold values from -6 to 6
- second_moment: float32 [4, 288, 16384], P('mp', 'dp'), may hold values from 0.05 to 2
- average_weights: float32 [4, 288, 16384], P('mp', 'dp'), may hold values from -6 to 6
Outputs:
- new_params: bfloat16 [4, 192, 16384], P('mp')
- new_master: float32 [4, 288, 16384], P('mp', 'dp')
- new_first: float32 [4, 288, 16384], P('mp', 'dp')
- new_second: float32 [4, 288, 16384], P('mp', 'dp')
- average_rows: float32 [4, 192, 16384], P('mp', 'dp')
The draws below stay inside these ranges and needn't reach their ends.
Inputs may be any that keep to these rules, and one draw needn't show every extreme that they name: `owner_list`: each data rank owns at most 36 segments, and some rank owns exactly 36.
All inputs are finite; a program needn't handle non-finite values.
Results may differ from the reference program's by a relative error of at most 0.015.
Values may be sent and summed in bfloat16 or wider, within the bound.
No kernel may reach another device: no remote copies, remote signals or barrier semaphores. Data moves between devices by JAX's collectives and lax.ppermute only.
A program may use at most 128 MiB of HBM per device.

```python
import math
import jax
import jax.numpy as jnp
from jax import lax

SEG = 16384
NSEG = 192
CAP = 36
N_DP = 8
N_MP = 4


def draw_gradients(key, part):
    subkeys = jax.random.split(key, 3)
    row_scale = jnp.exp(jax.random.uniform(subkeys[0], (1, N_MP, NSEG, 1), jnp.float32, 0.0, math.log(10.0)))
    col_scale = jnp.exp(jax.random.uniform(subkeys[1], (1, 1, 1, SEG), jnp.float32, 0.0, math.log(10.0)))
    rising = (3.0 ** (jnp.arange(N_MP, dtype=jnp.float32) / max(N_MP - 1, 1))).reshape(1, N_MP, 1, 1)
    values = jnp.clip(jax.random.normal(subkeys[2], (N_DP, N_MP, NSEG, SEG), jnp.float32), -6.0, 6.0)
    return (values * row_scale * col_scale * rising).astype(jnp.bfloat16)


def draw_owner_list(key, part):
    subkeys = jax.random.split(key, 3)
    first_rank = jax.random.randint(subkeys[0], (), 0, N_DP)
    order = jax.random.permutation(subkeys[1], NSEG)
    spare = jax.random.permutation(subkeys[2], (N_DP - 1) * CAP)[:NSEG - CAP]
    others = spare // CAP
    others = others + (others >= first_rank).astype(jnp.int32)
    by_position = jnp.concatenate([jnp.full((CAP,), first_rank, jnp.int32), others.astype(jnp.int32)])
    return jnp.zeros((NSEG,), jnp.int32).at[order].set(by_position)


def shard_levels(rng, extent, pieces, smallest, high):
    gain, own = 1.0, jax.random.fold_in(rng, 6)
    for dim, parts in pieces:
        heights = jnp.exp(jax.random.uniform(jax.random.fold_in(own, dim), (parts,), jnp.float32, smallest / len(pieces), high / len(pieces)))
        gain = gain * jnp.repeat(heights, extent[dim] // parts).reshape([-1 if axis == dim else 1 for axis in range(len(extent))])
    return gain


def scatter_about(key, extent, deviation, bound, pieces=(), kind=jnp.bfloat16):
    factor_of = shard_levels(key, extent, pieces, -0.22, 0.18) if pieces else 1.0
    drawn = jax.random.normal(key, extent, jnp.float32) * deviation * factor_of
    return jnp.minimum(jnp.maximum(drawn, -bound), bound).astype(kind)


def setup_inputs(seed: int = 0) -> dict:
    keys = jax.random.split(jax.random.key(seed), 7)
    return {
        "gradients": draw_gradients(jax.random.fold_in(keys[6], 71), 0),
        "owner_list": draw_owner_list(jax.random.fold_in(keys[6], 71), 0),
        "master_weights": scatter_about(keys[2], (N_MP, N_DP * CAP, SEG), 1.0, 6.0, ((0, 4), (1, 8)), jnp.float32),
        "first_moment": scatter_about(keys[3], (N_MP, N_DP * CAP, SEG), 1.0, 6.0, ((0, 4), (1, 8)), jnp.float32),
        "second_moment": jnp.clip(jnp.exp(math.log(2.0) - 3.6888794 * jax.random.uniform(keys[4], (N_MP, N_DP * CAP, SEG), jnp.float32) ** shard_levels(keys[4], (N_MP, N_DP * CAP, SEG), ((0, 4), (1, 8)), -0.2, 0.2)), 0.05, 2.0),
        "average_weights": scatter_about(keys[5], (N_MP, N_DP * CAP, SEG), 1.0, 6.0, ((0, 4), (1, 8)), jnp.float32),
    }


def slot_matrix(owner_list, ranks, cap):
    count = owner_list.shape[0]
    position = jnp.arange(count, dtype=jnp.int32)
    same_owner = (owner_list[:, None] == owner_list[None, :]) & (position[None, :] < position[:, None])
    slot_index = owner_list * cap + lax.optimization_barrier(jnp.sum(same_owner.astype(jnp.int32), axis=1))
    rows = jnp.arange(ranks * cap, dtype=jnp.int32)
    return (rows[:, None] == slot_index[None, :]).astype(jnp.float32)

def reference(gradients, owner_list, master_weights, first_moment, second_moment, average_weights):
    highest = lax.Precision.HIGHEST
    placing = slot_matrix(owner_list, N_DP, CAP)
    in_use = lax.optimization_barrier(jnp.sum(placing, axis=1))[None, :, None]

    def add_rank(source_rank, running):
        return running + gradients[source_rank].astype(jnp.float32)
    summed = lax.fori_loop(0, N_DP, add_rank, jnp.zeros((N_MP, NSEG, SEG), jnp.float32))
    norm_value = jnp.sqrt(jnp.sum(summed * summed))
    clip_factor = jnp.minimum(1.0, math.sqrt(N_MP * NSEG * SEG) / (norm_value + 1e-06))
    owned_grad = clip_factor * jnp.einsum('js,msc->mjc', placing, summed, precision=highest)
    new_first = in_use * (0.9 * first_moment + 0.1 * owned_grad)
    new_second = in_use * (0.95 * second_moment + 0.05 * owned_grad * owned_grad)
    first_hat = new_first / (1.0 - 0.9 ** 20)
    second_hat = new_second / (1.0 - 0.95 ** 20)
    new_master = in_use * (master_weights - 0.02 * (first_hat / (jnp.sqrt(second_hat) + 1e-08) + 0.1 * master_weights))
    averaged = 0.9 * average_weights + 0.1 * new_master
    new_params = jnp.einsum('js,mjc->msc', placing, new_master, precision=highest).astype(jnp.bfloat16)
    average_rows = jnp.einsum('js,mjc->msc', placing, averaged, precision=highest)
    return (new_params, new_master, new_first, new_second, average_rows)
```

```python
import math

import jax
import jax.numpy as jnp
from jax import lax
from jax.sharding import PartitionSpec as P


def ring_order(mesh):
    n = mesh.shape["dp"]
    try:
        coords = [tuple(mesh.devices[i, 0].coords) for i in range(n)]
        at = {(c[2], c[1]): i for i, c in enumerate(coords)}
        zs = sorted({z for z, _ in at})
        ys = sorted({y for _, y in at})
        if len(at) != n or len(zs) * len(ys) != n:
            return list(range(n))
        if len(ys) % 2:
            if len(zs) % 2:
                return list(range(n))
            at = {(y, z): i for (z, y), i in at.items()}
            zs, ys = ys, zs
        if len(zs) == 1 or len(ys) == 1:
            line = zs if len(ys) == 1 else ys
            return [at[(z, ys[0])] if len(ys) == 1 else at[(zs[0], z)] for z in line]
        cycle = [(z, ys[0]) for z in zs]
        for k, y in enumerate(ys[1:]):
            inner = zs[1:][::-1] if k % 2 == 0 else zs[1:]
            cycle += [(z, y) for z in inner]
        cycle += [(zs[0], y) for y in ys[1:][::-1]]
        return [at[c] for c in cycle]
    except (AttributeError, TypeError, IndexError, KeyError):
        return list(range(n))


def make_on_device(ring):
    n = len(ring)
    pos_of = [ring.index(r) for r in range(n)]
    fwd = [(ring[q], ring[(q + 1) % n]) for q in range(n)]
    bwd = [(ring[(q + 1) % n], ring[q]) for q in range(n)]

    def on_device(gradients, owner_list, master_weights, first_moment, second_moment, average_weights):
        local_grad = gradients[0, 0]
        nseg, seg = local_grad.shape
        cap = master_weights.shape[1]
        blocks = lax.axis_size("mp")
        per_rank = nseg // n
        half = seg // 2
        me = lax.axis_index("dp")
        rank_at = jnp.array(ring, jnp.int32)
        mypos = jnp.array(pos_of, jnp.int32)[me]

        position = jnp.arange(nseg, dtype=jnp.int32)
        same_owner = (owner_list[:, None] == owner_list[None, :]) & (position[None, :] < position[:, None])
        within = jnp.sum(same_owner.astype(jnp.int32), axis=1)
        slot = owner_list * cap + within
        hit = jnp.arange(n * cap, dtype=jnp.int32)[:, None] == slot[None, :]
        valid = jnp.any(hit, axis=1)
        seg_of_slot = jnp.sum(jnp.where(hit, position[None, :], 0), axis=1)
        by_owner = jnp.where(
            valid[:, None], jnp.take(local_grad, seg_of_slot, axis=0), jnp.zeros((), local_grad.dtype)
        ).reshape(n, cap, seg)
        left, right = by_owner[..., :half], by_owner[..., half:]

        def own(x, p):
            return lax.dynamic_index_in_dim(x, rank_at[p % n], 0, keepdims=False).astype(jnp.float32)

        send_a = own(left, mypos - 1 + n).astype(jnp.bfloat16)
        send_b = own(right, mypos + 1).astype(jnp.bfloat16)
        for t in range(n - 1):
            got_a = lax.ppermute(send_a, "dp", fwd)
            got_b = lax.ppermute(send_b, "dp", bwd)
            acc_a = got_a.astype(jnp.float32) + own(left, mypos - 2 - t + 2 * n)
            acc_b = got_b.astype(jnp.float32) + own(right, mypos + 2 + t)
            if t < n - 2:
                send_a, send_b = acc_a.astype(jnp.bfloat16), acc_b.astype(jnp.bfloat16)
        owned = jnp.concatenate([acc_a, acc_b], axis=1)

        total_sq = lax.psum(jnp.sum(owned * owned), ("dp", "mp"))
        clip_factor = jnp.minimum(1.0, math.sqrt(blocks * nseg * seg) / (jnp.sqrt(total_sq) + 1e-06))
        in_use = lax.dynamic_index_in_dim(valid.reshape(n, cap), me, 0, keepdims=False)
        in_use = in_use.astype(jnp.float32)[:, None]
        owned_grad = clip_factor * owned
        new_first = in_use * (0.9 * first_moment[0] + 0.1 * owned_grad)
        new_second = in_use * (0.95 * second_moment[0] + 0.05 * owned_grad * owned_grad)
        first_hat = new_first / (1.0 - 0.9**20)
        second_hat = new_second / (1.0 - 0.95**20)
        old_master = master_weights[0]
        new_master = in_use * (
            old_master - 0.02 * (first_hat / (jnp.sqrt(second_hat) + 1e-08) + 0.1 * old_master)
        )
        averaged = 0.9 * average_weights[0] + 0.1 * new_master

        payload = jnp.concatenate([new_master, averaged], axis=0).astype(jnp.bfloat16)
        send_a, send_b = payload[:, :half], payload[:, half:]
        from_a, from_b = [], []
        for t in range(n - 1):
            send_a = lax.ppermute(send_a, "dp", fwd)
            send_b = lax.ppermute(send_b, "dp", bwd)
            from_a.append(send_a)
            from_b.append(send_b)
        all_a = jnp.stack([payload[:, :half]] + from_a[::-1]).reshape(n * 2 * cap, half)
        all_b = jnp.stack([payload[:, half:]] + from_b).reshape(n * 2 * cap, half)

        ahead = (jnp.array(pos_of, jnp.int32)[owner_list] - mypos + n) % n
        row = ahead * (2 * cap) + within
        new_params = jnp.concatenate(
            [jnp.take(all_a, row, axis=0), jnp.take(all_b, row, axis=0)], axis=1
        )
        mine = lax.dynamic_slice_in_dim(row, me * per_rank, per_rank) + cap
        average_rows = jnp.concatenate(
            [jnp.take(all_a, mine, axis=0), jnp.take(all_b, mine, axis=0)], axis=1
        ).astype(jnp.float32)
        return (
            new_params[None],
            new_master[None],
            new_first[None],
            new_second[None],
            average_rows[None],
        )

    return on_device


def solution(mesh):
    return jax.shard_map(
        make_on_device(ring_order(mesh)),
        mesh=mesh,
        in_specs=(
            P("dp", "mp", None, None),
            P(),
            P("mp", "dp", None),
            P("mp", "dp", None),
            P("mp", "dp", None),
            P("mp", "dp", None),
        ),
        out_specs=(
            P("mp", None, None),
            P("mp", "dp", None),
            P("mp", "dp", None),
            P("mp", "dp", None),
            P("mp", "dp", None),
        ),
        check_vma=False,
    )
```

```python
import math

import jax
import jax.numpy as jnp
from jax import lax
from jax.sharding import PartitionSpec as P


def ring_order(mesh):
    n = mesh.shape["dp"]
    try:
        coords = [tuple(mesh.devices[i, 0].coords) for i in range(n)]
        at = {(c[2], c[1]): i for i, c in enumerate(coords)}
        zs = sorted({z for z, _ in at})
        ys = sorted({y for _, y in at})
        if len(at) != n or len(zs) * len(ys) != n:
            return list(range(n))
        if len(ys) % 2:
            if len(zs) % 2:
                return list(range(n))
            at = {(y, z): i for (z, y), i in at.items()}
            zs, ys = ys, zs
        if len(zs) == 1 or len(ys) == 1:
            line = zs if len(ys) == 1 else ys
            return [at[(z, ys[0])] if len(ys) == 1 else at[(zs[0], z)] for z in line]
        cycle = [(z, ys[0]) for z in zs]
        for k, y in enumerate(ys[1:]):
            inner = zs[1:][::-1] if k % 2 == 0 else zs[1:]
            cycle += [(z, y) for z in inner]
        cycle += [(zs[0], y) for y in ys[1:][::-1]]
        return [at[c] for c in cycle]
    except (AttributeError, TypeError, IndexError, KeyError):
        return list(range(n))


def all_sum(v, axis, n):
    if n & (n - 1):
        return lax.psum(v, axis)
    k = 1
    while k < n:
        v = v + lax.ppermute(v, axis, [(i, i ^ k) for i in range(n)])
        k *= 2
    return v


def make_on_device(ring):
    n = len(ring)
    pos_of = [ring.index(r) for r in range(n)]
    fwd = [(ring[q], ring[(q + 1) % n]) for q in range(n)]
    bwd = [(ring[(q + 1) % n], ring[q]) for q in range(n)]

    def on_device(gradients, owner_list, master_weights, first_moment, second_moment, average_weights):
        local_grad = gradients[0, 0]
        nseg, seg = local_grad.shape
        cap = master_weights.shape[1]
        blocks = lax.axis_size("mp")
        per_rank = nseg // n
        half = seg // 2
        me = lax.axis_index("dp")
        rank_at = jnp.array(ring, jnp.int32)
        mypos = jnp.array(pos_of, jnp.int32)[me]

        position = jnp.arange(nseg, dtype=jnp.int32)
        same_owner = (owner_list[:, None] == owner_list[None, :]) & (position[None, :] < position[:, None])
        within = jnp.sum(same_owner.astype(jnp.int32), axis=1)
        slot = owner_list * cap + within
        hit = jnp.arange(n * cap, dtype=jnp.int32)[:, None] == slot[None, :]
        valid = jnp.any(hit, axis=1)
        placing = hit.astype(local_grad.dtype)
        left, right = local_grad[:, :half], local_grad[:, half:]

        def own(x, p):
            rows = lax.dynamic_slice_in_dim(placing, rank_at[p % n] * cap, cap, 0)
            return jnp.dot(rows, x, preferred_element_type=jnp.float32)

        send_a = own(left, mypos - 1 + n).astype(jnp.bfloat16)
        send_b = own(right, mypos + 1).astype(jnp.bfloat16)
        for t in range(n - 1):
            got_a = lax.ppermute(send_a, "dp", fwd)
            got_b = lax.ppermute(send_b, "dp", bwd)
            acc_a = got_a.astype(jnp.float32) + own(left, mypos - 2 - t + 2 * n)
            acc_b = got_b.astype(jnp.float32) + own(right, mypos + 2 + t)
            if t < n - 2:
                send_a, send_b = acc_a.astype(jnp.bfloat16), acc_b.astype(jnp.bfloat16)
        owned = jnp.concatenate([acc_a, acc_b], axis=1)

        total_sq = all_sum(all_sum(jnp.sum(owned * owned).reshape(1, 1), "dp", n), "mp", blocks)[0, 0]
        clip_factor = jnp.minimum(1.0, math.sqrt(blocks * nseg * seg) / (jnp.sqrt(total_sq) + 1e-06))
        in_use = lax.dynamic_index_in_dim(valid.reshape(n, cap), me, 0, keepdims=False)
        in_use = in_use.astype(jnp.float32)[:, None]
        owned_grad = clip_factor * owned
        new_first = in_use * (0.9 * first_moment[0] + 0.1 * owned_grad)
        new_second = in_use * (0.95 * second_moment[0] + 0.05 * owned_grad * owned_grad)
        first_hat = new_first / (1.0 - 0.9**20)
        second_hat = new_second / (1.0 - 0.95**20)
        old_master = master_weights[0]
        new_master = in_use * (
            old_master - 0.02 * (first_hat / (jnp.sqrt(second_hat) + 1e-08) + 0.1 * old_master)
        )
        averaged = 0.9 * average_weights[0] + 0.1 * new_master

        payload = jnp.concatenate([new_master, averaged], axis=0).astype(jnp.bfloat16)
        send_a, send_b = payload[:, :half], payload[:, half:]
        placing_t = placing.T
        mine_t = lax.dynamic_slice_in_dim(placing_t, me * per_rank, per_rank, 0)

        def spread(rows_t, chunk, p, kind):
            cols = lax.dynamic_slice_in_dim(rows_t, rank_at[p % n] * cap, cap, 1)
            return jnp.dot(cols, chunk, preferred_element_type=kind)

        def place(acc, p_a, a, p_b, b):
            parts = (
                spread(placing_t, a[:cap], p_a, jnp.bfloat16),
                spread(placing_t, b[:cap], p_b, jnp.bfloat16),
                spread(mine_t, a[cap:], p_a, jnp.float32),
                spread(mine_t, b[cap:], p_b, jnp.float32),
            )
            if acc is None:
                return parts
            return tuple(x + y for x, y in zip(acc, parts))

        acc = place(None, mypos, send_a, mypos, send_b)
        for t in range(n - 1):
            send_a = lax.ppermute(send_a, "dp", fwd)
            send_b = lax.ppermute(send_b, "dp", bwd)
            acc = place(acc, mypos - 1 - t + n, send_a, mypos + 1 + t, send_b)
        new_params = jnp.concatenate([acc[0], acc[1]], axis=1)
        average_rows = jnp.concatenate([acc[2], acc[3]], axis=1)
        return (
            new_params[None],
            new_master[None],
            new_first[None],
            new_second[None],
            average_rows[None],
        )

    return on_device


def solution(mesh):
    return jax.shard_map(
        make_on_device(ring_order(mesh)),
        mesh=mesh,
        in_specs=(
            P("dp", "mp", None, None),
            P(),
            P("mp", "dp", None),
            P("mp", "dp", None),
            P("mp", "dp", None),
            P("mp", "dp", None),
        ),
        out_specs=(
            P("mp", None, None),
            P("mp", "dp", None),
            P("mp", "dp", None),
            P("mp", "dp", None),
            P("mp", "dp", None),
        ),
        check_vma=False,
    )
```

```python
import math

import jax
import jax.numpy as jnp
from jax import lax
from jax.sharding import PartitionSpec as P


def ring_order(mesh):
    n = mesh.shape["dp"]
    try:
        coords = [tuple(mesh.devices[i, 0].coords) for i in range(n)]
        at = {(c[2], c[1]): i for i, c in enumerate(coords)}
        zs = sorted({z for z, _ in at})
        ys = sorted({y for _, y in at})
        if len(at) != n or len(zs) * len(ys) != n:
            return list(range(n))
        if len(ys) % 2:
            if len(zs) % 2:
                return list(range(n))
            at = {(y, z): i for (z, y), i in at.items()}
            zs, ys = ys, zs
        if len(zs) == 1 or len(ys) == 1:
            line = zs if len(ys) == 1 else ys
            return [at[(z, ys[0])] if len(ys) == 1 else at[(zs[0], z)] for z in line]
        cycle = [(z, ys[0]) for z in zs]
        for k, y in enumerate(ys[1:]):
            inner = zs[1:][::-1] if k % 2 == 0 else zs[1:]
            cycle += [(z, y) for z in inner]
        cycle += [(zs[0], y) for y in ys[1:][::-1]]
        return [at[c] for c in cycle]
    except (AttributeError, TypeError, IndexError, KeyError):
        return list(range(n))


def all_sum(v, axis, n):
    if n & (n - 1):
        return lax.psum(v, axis)
    k = 1
    while k < n:
        v = v + lax.ppermute(v, axis, [(i, i ^ k) for i in range(n)])
        k *= 2
    return v


def make_on_device(ring):
    n = len(ring)
    pos_of = [ring.index(r) for r in range(n)]
    fwd = [(ring[q], ring[(q + 1) % n]) for q in range(n)]
    bwd = [(ring[(q + 1) % n], ring[q]) for q in range(n)]

    def on_device(gradients, owner_list, master_weights, first_moment, second_moment, average_weights):
        local_grad = gradients[0, 0]
        nseg, seg = local_grad.shape
        cap = master_weights.shape[1]
        blocks = lax.axis_size("mp")
        per_rank = nseg // n
        half = seg // 2
        me = lax.axis_index("dp")
        rank_at = jnp.array(ring, jnp.int32)
        mypos = jnp.array(pos_of, jnp.int32)[me]

        position = jnp.arange(nseg, dtype=jnp.int32)
        same_owner = (owner_list[:, None] == owner_list[None, :]) & (position[None, :] < position[:, None])
        within = jnp.sum(same_owner.astype(jnp.int32), axis=1)
        slot = owner_list * cap + within
        hit = jnp.arange(n * cap, dtype=jnp.int32)[:, None] == slot[None, :]
        valid = jnp.any(hit, axis=1)
        placing = hit.astype(local_grad.dtype)
        by_owner = jnp.dot(placing, local_grad, preferred_element_type=jnp.bfloat16).reshape(n, cap, seg)
        left, right = by_owner[..., :half], by_owner[..., half:]

        def own(x, p):
            return lax.dynamic_index_in_dim(x, rank_at[p % n], 0, keepdims=False).astype(jnp.float32)

        send_a = own(left, mypos - 1 + n).astype(jnp.bfloat16)
        send_b = own(right, mypos + 1).astype(jnp.bfloat16)
        for t in range(n - 1):
            got_a = lax.ppermute(send_a, "dp", fwd)
            got_b = lax.ppermute(send_b, "dp", bwd)
            acc_a = got_a.astype(jnp.float32) + own(left, mypos - 2 - t + 2 * n)
            acc_b = got_b.astype(jnp.float32) + own(right, mypos + 2 + t)
            if t < n - 2:
                send_a, send_b = acc_a.astype(jnp.bfloat16), acc_b.astype(jnp.bfloat16)
        owned = jnp.concatenate([acc_a, acc_b], axis=1)

        total_sq = all_sum(all_sum(jnp.sum(owned * owned).reshape(1, 1), "dp", n), "mp", blocks)[0, 0]
        clip_factor = jnp.minimum(1.0, math.sqrt(blocks * nseg * seg) / (jnp.sqrt(total_sq) + 1e-06))
        in_use = lax.dynamic_index_in_dim(valid.reshape(n, cap), me, 0, keepdims=False)
        in_use = in_use.astype(jnp.float32)[:, None]
        owned_grad = clip_factor * owned
        new_first = in_use * (0.9 * first_moment[0] + 0.1 * owned_grad)
        new_second = in_use * (0.95 * second_moment[0] + 0.05 * owned_grad * owned_grad)
        first_hat = new_first / (1.0 - 0.9**20)
        second_hat = new_second / (1.0 - 0.95**20)
        old_master = master_weights[0]
        new_master = in_use * (
            old_master - 0.02 * (first_hat / (jnp.sqrt(second_hat) + 1e-08) + 0.1 * old_master)
        )
        averaged = 0.9 * average_weights[0] + 0.1 * new_master

        payload = jnp.concatenate([new_master, averaged], axis=0).astype(jnp.bfloat16)
        send_a, send_b = payload[:, :half], payload[:, half:]
        placing_t = placing.T
        mine_t = lax.dynamic_slice_in_dim(placing_t, me * per_rank, per_rank, 0)

        def spread(rows_t, chunk, p, kind):
            cols = lax.dynamic_slice_in_dim(rows_t, rank_at[p % n] * cap, cap, 1)
            return jnp.dot(cols, chunk, preferred_element_type=kind)

        def place(acc, p_a, a, p_b, b):
            parts = (
                spread(placing_t, a[:cap], p_a, jnp.bfloat16),
                spread(placing_t, b[:cap], p_b, jnp.bfloat16),
                spread(mine_t, a[cap:], p_a, jnp.float32),
                spread(mine_t, b[cap:], p_b, jnp.float32),
            )
            if acc is None:
                return parts
            return tuple(x + y for x, y in zip(acc, parts))

        acc = place(None, mypos, send_a, mypos, send_b)
        for t in range(n - 1):
            send_a = lax.ppermute(send_a, "dp", fwd)
            send_b = lax.ppermute(send_b, "dp", bwd)
            acc = place(acc, mypos - 1 - t + n, send_a, mypos + 1 + t, send_b)
        new_params = jnp.concatenate([acc[0], acc[1]], axis=1)
        average_rows = jnp.concatenate([acc[2], acc[3]], axis=1)
        return (
            new_params[None],
            new_master[None],
            new_first[None],
            new_second[None],
            average_rows[None],
        )

    return on_device


def solution(mesh):
    return jax.shard_map(
        make_on_device(ring_order(mesh)),
        mesh=mesh,
        in_specs=(
            P("dp", "mp", None, None),
            P(),
            P("mp", "dp", None),
            P("mp", "dp", None),
            P("mp", "dp", None),
            P("mp", "dp", None),
        ),
        out_specs=(
            P("mp", None, None),
            P("mp", "dp", None),
            P("mp", "dp", None),
            P("mp", "dp", None),
            P("mp", "dp", None),
        ),
        check_vma=False,
    )
```

```python
import math

import jax
import jax.numpy as jnp
from jax import lax
from jax.sharding import PartitionSpec as P


def ring_order(mesh):
    n = mesh.shape["dp"]
    try:
        coords = [tuple(mesh.devices[i, 0].coords) for i in range(n)]
        at = {(c[2], c[1]): i for i, c in enumerate(coords)}
        zs = sorted({z for z, _ in at})
        ys = sorted({y for _, y in at})
        if len(at) != n or len(zs) * len(ys) != n:
            return list(range(n))
        if len(ys) % 2:
            if len(zs) % 2:
                return list(range(n))
            at = {(y, z): i for (z, y), i in at.items()}
            zs, ys = ys, zs
        if len(zs) == 1 or len(ys) == 1:
            line = zs if len(ys) == 1 else ys
            return [at[(z, ys[0])] if len(ys) == 1 else at[(zs[0], z)] for z in line]
        cycle = [(z, ys[0]) for z in zs]
        for k, y in enumerate(ys[1:]):
            inner = zs[1:][::-1] if k % 2 == 0 else zs[1:]
            cycle += [(z, y) for z in inner]
        cycle += [(zs[0], y) for y in ys[1:][::-1]]
        return [at[c] for c in cycle]
    except (AttributeError, TypeError, IndexError, KeyError):
        return list(range(n))


def all_sum(v, axis, n):
    if n & (n - 1):
        return lax.psum(v, axis)
    k = 1
    while k < n:
        v = v + lax.ppermute(v, axis, [(i, i ^ k) for i in range(n)])
        k *= 2
    return v


def make_on_device(ring):
    n = len(ring)
    pos_of = [ring.index(r) for r in range(n)]
    fwd = [(ring[q], ring[(q + 1) % n]) for q in range(n)]
    bwd = [(ring[(q + 1) % n], ring[q]) for q in range(n)]

    def on_device(gradients, owner_list, master_weights, first_moment, second_moment, average_weights):
        local_grad = gradients[0, 0]
        nseg, seg = local_grad.shape
        cap = master_weights.shape[1]
        blocks = lax.axis_size("mp")
        per_rank = nseg // n
        half = seg // 2
        me = lax.axis_index("dp")
        mypos = jnp.array(pos_of, jnp.int32)[me]

        warm = jnp.zeros((8, 128), jnp.bfloat16)
        warm = lax.ppermute(warm, "dp", fwd) + lax.ppermute(warm, "dp", bwd)

        position = jnp.arange(nseg, dtype=jnp.int32)
        same_owner = (owner_list[:, None] == owner_list[None, :]) & (position[None, :] < position[:, None])
        within = jnp.sum(same_owner.astype(jnp.int32), axis=1)
        ahead = (jnp.array(pos_of, jnp.int32)[owner_list] - mypos + n) % n
        slot = ahead * cap + within
        hit = jnp.arange(n * cap, dtype=jnp.int32)[:, None] == slot[None, :]
        valid = jnp.any(hit[:cap], axis=1)
        placing = hit.astype(local_grad.dtype)
        left = jnp.dot(placing, local_grad[:, :half], preferred_element_type=jnp.bfloat16).reshape(n, cap, half)
        right = jnp.dot(placing, local_grad[:, half:], preferred_element_type=jnp.bfloat16).reshape(n, cap, half)

        send_a = left[n - 1] + warm[:1, :1]
        send_b = right[1]
        for t in range(n - 1):
            got_a = lax.ppermute(send_a, "dp", fwd)
            got_b = lax.ppermute(send_b, "dp", bwd)
            acc_a = got_a.astype(jnp.float32) + left[(2 * n - 2 - t) % n].astype(jnp.float32)
            acc_b = got_b.astype(jnp.float32) + right[(2 + t) % n].astype(jnp.float32)
            if t < n - 2:
                send_a, send_b = acc_a.astype(jnp.bfloat16), acc_b.astype(jnp.bfloat16)
        owned = jnp.concatenate([acc_a, acc_b], axis=1)

        total_sq = all_sum(all_sum(jnp.sum(owned * owned).reshape(1, 1), "dp", n), "mp", blocks)[0, 0]
        clip_factor = jnp.minimum(1.0, math.sqrt(blocks * nseg * seg) / (jnp.sqrt(total_sq) + 1e-06))
        in_use = valid.astype(jnp.float32)[:, None]
        owned_grad = clip_factor * owned
        new_first = in_use * (0.9 * first_moment[0] + 0.1 * owned_grad)
        new_second = in_use * (0.95 * second_moment[0] + 0.05 * owned_grad * owned_grad)
        first_hat = new_first / (1.0 - 0.9**20)
        second_hat = new_second / (1.0 - 0.95**20)
        old_master = master_weights[0]
        new_master = in_use * (
            old_master - 0.02 * (first_hat / (jnp.sqrt(second_hat) + 1e-08) + 0.1 * old_master)
        )
        averaged = 0.9 * average_weights[0] + 0.1 * new_master

        payload = jnp.concatenate([new_master, averaged], axis=0).astype(jnp.bfloat16)
        send_a, send_b = payload[:, :half], payload[:, half:]
        placing_t = placing.T
        mine_t = lax.dynamic_slice_in_dim(placing_t, me * per_rank, per_rank, 0)

        def spread(rows_t, chunk, k, kind):
            return jnp.dot(rows_t[:, k * cap:(k + 1) * cap], chunk, preferred_element_type=kind)

        def place(acc, k_a, a, k_b, b):
            parts = (
                spread(placing_t, a[:cap], k_a, jnp.bfloat16),
                spread(placing_t, b[:cap], k_b, jnp.bfloat16),
                spread(mine_t, a[cap:], k_a, jnp.float32),
                spread(mine_t, b[cap:], k_b, jnp.float32),
            )
            if acc is None:
                return parts
            return tuple(x + y for x, y in zip(acc, parts))

        acc = place(None, 0, send_a, 0, send_b)
        for t in range(n - 1):
            send_a = lax.ppermute(send_a, "dp", fwd)
            send_b = lax.ppermute(send_b, "dp", bwd)
            acc = place(acc, n - 1 - t, send_a, 1 + t, send_b)
        new_params = jnp.concatenate([acc[0], acc[1]], axis=1)
        average_rows = jnp.concatenate([acc[2], acc[3]], axis=1)
        return (
            new_params[None],
            new_master[None],
            new_first[None],
            new_second[None],
            average_rows[None],
        )

    return on_device


def solution(mesh):
    return jax.shard_map(
        make_on_device(ring_order(mesh)),
        mesh=mesh,
        in_specs=(
            P("dp", "mp", None, None),
            P(),
            P("mp", "dp", None),
            P("mp", "dp", None),
            P("mp", "dp", None),
            P("mp", "dp", None),
        ),
        out_specs=(
            P("mp", None, None),
            P("mp", "dp", None),
            P("mp", "dp", None),
            P("mp", "dp", None),
            P("mp", "dp", None),
        ),
        check_vma=False,
    )
```

```python
import math

import jax
import jax.numpy as jnp
from jax import lax
from jax.sharding import PartitionSpec as P


def ring_order(mesh):
    n = mesh.shape["dp"]
    try:
        coords = [tuple(mesh.devices[i, 0].coords) for i in range(n)]
        at = {(c[2], c[1]): i for i, c in enumerate(coords)}
        zs = sorted({z for z, _ in at})
        ys = sorted({y for _, y in at})
        if len(at) != n or len(zs) * len(ys) != n:
            return list(range(n))
        if len(ys) % 2:
            if len(zs) % 2:
                return list(range(n))
            at = {(y, z): i for (z, y), i in at.items()}
            zs, ys = ys, zs
        if len(zs) == 1 or len(ys) == 1:
            line = zs if len(ys) == 1 else ys
            return [at[(z, ys[0])] if len(ys) == 1 else at[(zs[0], z)] for z in line]
        cycle = [(z, ys[0]) for z in zs]
        for k, y in enumerate(ys[1:]):
            inner = zs[1:][::-1] if k % 2 == 0 else zs[1:]
            cycle += [(z, y) for z in inner]
        cycle += [(zs[0], y) for y in ys[1:][::-1]]
        return [at[c] for c in cycle]
    except (AttributeError, TypeError, IndexError, KeyError):
        return list(range(n))


def all_sum(v, axis, n):
    if n & (n - 1):
        return lax.psum(v, axis)
    k = 1
    while k < n:
        v = v + lax.ppermute(v, axis, [(i, i ^ k) for i in range(n)])
        k *= 2
    return v


def make_on_device(ring):
    n = len(ring)
    pos_of = [ring.index(r) for r in range(n)]
    fwd = [(ring[q], ring[(q + 1) % n]) for q in range(n)]
    bwd = [(ring[(q + 1) % n], ring[q]) for q in range(n)]

    def on_device(gradients, owner_list, master_weights, first_moment, second_moment, average_weights):
        local_grad = gradients[0, 0]
        nseg, seg = local_grad.shape
        cap = master_weights.shape[1]
        blocks = lax.axis_size("mp")
        per_rank = nseg // n
        half = seg // 2
        me = lax.axis_index("dp")
        mypos = jnp.array(pos_of, jnp.int32)[me]

        warm = jnp.zeros((8, 128), jnp.bfloat16)
        warm = lax.ppermute(warm, "dp", fwd) + lax.ppermute(warm, "dp", bwd)

        position = jnp.arange(nseg, dtype=jnp.int32)
        same_owner = (owner_list[:, None] == owner_list[None, :]) & (position[None, :] < position[:, None])
        within = jnp.sum(same_owner.astype(jnp.int32), axis=1)
        ahead = (jnp.array(pos_of, jnp.int32)[owner_list] - mypos + n) % n
        slot = ahead * cap + within
        hit = jnp.arange(n * cap, dtype=jnp.int32)[:, None] == slot[None, :]
        valid = jnp.any(hit[:cap], axis=1)
        placing = hit.astype(local_grad.dtype)
        left = jnp.dot(placing, local_grad[:, :half], preferred_element_type=jnp.bfloat16).reshape(n, cap, half)
        right = jnp.dot(placing, local_grad[:, half:], preferred_element_type=jnp.bfloat16).reshape(n, cap, half)

        placing_t = placing.T
        mine_t = lax.dynamic_slice_in_dim(placing_t, me * per_rank, per_rank, 0)

        def spread(rows_t, chunk, k, kind):
            return jnp.dot(rows_t[:, k * cap:(k + 1) * cap], chunk, preferred_element_type=kind)

        old_avg = average_weights[0].astype(jnp.bfloat16)
        w_a, w_b = old_avg[:, :half], old_avg[:, half:]
        avg_a = spread(mine_t, w_a, 0, jnp.float32)
        avg_b = spread(mine_t, w_b, 0, jnp.float32)
        send_a = left[n - 1] + warm[:1, :1]
        send_b = right[1]
        for t in range(n - 1):
            got_a = lax.ppermute(send_a, "dp", fwd)
            got_b = lax.ppermute(send_b, "dp", bwd)
            w_a = lax.ppermute(w_a, "dp", fwd)
            w_b = lax.ppermute(w_b, "dp", bwd)
            acc_a = got_a.astype(jnp.float32) + left[(2 * n - 2 - t) % n].astype(jnp.float32)
            acc_b = got_b.astype(jnp.float32) + right[(2 + t) % n].astype(jnp.float32)
            if t < n - 2:
                send_a, send_b = acc_a.astype(jnp.bfloat16), acc_b.astype(jnp.bfloat16)
                send_a, send_b, w_a, w_b = lax.optimization_barrier((send_a, send_b, w_a, w_b))
            avg_a = avg_a + spread(mine_t, w_a, n - 1 - t, jnp.float32)
            avg_b = avg_b + spread(mine_t, w_b, 1 + t, jnp.float32)
        owned = jnp.concatenate([acc_a, acc_b], axis=1)

        total_sq = all_sum(all_sum(jnp.sum(owned * owned).reshape(1, 1), "dp", n), "mp", blocks)[0, 0]
        clip_factor = jnp.minimum(1.0, math.sqrt(blocks * nseg * seg) / (jnp.sqrt(total_sq) + 1e-06))
        in_use = valid.astype(jnp.float32)[:, None]
        owned_grad = clip_factor * owned
        new_first = in_use * (0.9 * first_moment[0] + 0.1 * owned_grad)
        new_second = in_use * (0.95 * second_moment[0] + 0.05 * owned_grad * owned_grad)
        first_hat = new_first / (1.0 - 0.9**20)
        second_hat = new_second / (1.0 - 0.95**20)
        old_master = master_weights[0]
        new_master = in_use * (
            old_master - 0.02 * (first_hat / (jnp.sqrt(second_hat) + 1e-08) + 0.1 * old_master)
        )

        payload = new_master.astype(jnp.bfloat16)
        send_a, send_b = payload[:, :half], payload[:, half:]

        def place(acc, k_a, a, k_b, b):
            parts = (
                spread(placing_t, a, k_a, jnp.bfloat16),
                spread(placing_t, b, k_b, jnp.bfloat16),
                spread(mine_t, a, k_a, jnp.float32),
                spread(mine_t, b, k_b, jnp.float32),
            )
            if acc is None:
                return parts
            return tuple(x + y for x, y in zip(acc, parts))

        acc = place(None, 0, send_a, 0, send_b)
        for t in range(n - 1):
            send_a = lax.ppermute(send_a, "dp", fwd)
            send_b = lax.ppermute(send_b, "dp", bwd)
            acc = place(acc, n - 1 - t, send_a, 1 + t, send_b)
        new_params = jnp.concatenate([acc[0], acc[1]], axis=1)
        average_rows = jnp.concatenate(
            [0.9 * avg_a + 0.1 * acc[2], 0.9 * avg_b + 0.1 * acc[3]], axis=1
        )
        return (
            new_params[None],
            new_master[None],
            new_first[None],
            new_second[None],
            average_rows[None],
        )

    return on_device


def solution(mesh):
    return jax.shard_map(
        make_on_device(ring_order(mesh)),
        mesh=mesh,
        in_specs=(
            P("dp", "mp", None, None),
            P(),
            P("mp", "dp", None),
            P("mp", "dp", None),
            P("mp", "dp", None),
            P("mp", "dp", None),
        ),
        out_specs=(
            P("mp", None, None),
            P("mp", "dp", None),
            P("mp", "dp", None),
            P("mp", "dp", None),
            P("mp", "dp", None),
        ),
        check_vma=False,
    )
```

```python
import math

import jax
import jax.numpy as jnp
from jax import lax
from jax.sharding import PartitionSpec as P


def ring_order(mesh):
    n = mesh.shape["dp"]
    try:
        coords = [tuple(mesh.devices[i, 0].coords) for i in range(n)]
        at = {(c[2], c[1]): i for i, c in enumerate(coords)}
        zs = sorted({z for z, _ in at})
        ys = sorted({y for _, y in at})
        if len(at) != n or len(zs) * len(ys) != n:
            return list(range(n))
        if len(ys) % 2:
            if len(zs) % 2:
                return list(range(n))
            at = {(y, z): i for (z, y), i in at.items()}
            zs, ys = ys, zs
        if len(zs) == 1 or len(ys) == 1:
            line = zs if len(ys) == 1 else ys
            return [at[(z, ys[0])] if len(ys) == 1 else at[(zs[0], z)] for z in line]
        cycle = [(z, ys[0]) for z in zs]
        for k, y in enumerate(ys[1:]):
            inner = zs[1:][::-1] if k % 2 == 0 else zs[1:]
            cycle += [(z, y) for z in inner]
        cycle += [(zs[0], y) for y in ys[1:][::-1]]
        return [at[c] for c in cycle]
    except (AttributeError, TypeError, IndexError, KeyError):
        return list(range(n))


def all_sum(v, axis, n):
    if n & (n - 1):
        return lax.psum(v, axis)
    k = 1
    while k < n:
        v = v + lax.ppermute(v, axis, [(i, i ^ k) for i in range(n)])
        k *= 2
    return v


def make_on_device(ring):
    n = len(ring)
    pos_of = [ring.index(r) for r in range(n)]
    fwd = [(ring[q], ring[(q + 1) % n]) for q in range(n)]
    bwd = [(ring[(q + 1) % n], ring[q]) for q in range(n)]

    def on_device(gradients, owner_list, master_weights, first_moment, second_moment, average_weights):
        local_grad = gradients[0, 0]
        nseg, seg = local_grad.shape
        cap = master_weights.shape[1]
        blocks = lax.axis_size("mp")
        per_rank = nseg // n
        half = seg // 2
        me = lax.axis_index("dp")
        mypos = jnp.array(pos_of, jnp.int32)[me]

        warm = jnp.zeros((8, 128), jnp.bfloat16)
        warm = lax.ppermute(warm, "dp", fwd) + lax.ppermute(warm, "dp", bwd)

        position = jnp.arange(nseg, dtype=jnp.int32)
        same_owner = (owner_list[:, None] == owner_list[None, :]) & (position[None, :] < position[:, None])
        within = jnp.sum(same_owner.astype(jnp.int32), axis=1)
        ahead = (jnp.array(pos_of, jnp.int32)[owner_list] - mypos + n) % n
        slot = ahead * cap + within
        hit = jnp.arange(n * cap, dtype=jnp.int32)[:, None] == slot[None, :]
        valid = jnp.any(hit[:cap], axis=1)
        placing = hit.astype(local_grad.dtype)
        left = jnp.dot(placing, local_grad[:, :half], preferred_element_type=jnp.bfloat16).reshape(n, cap, half)
        right = jnp.dot(placing, local_grad[:, half:], preferred_element_type=jnp.bfloat16).reshape(n, cap, half)

        send_a = left[n - 1] + warm[:1, :1]
        send_b = right[1]
        for t in range(n - 1):
            got_a = lax.ppermute(send_a, "dp", fwd)
            got_b = lax.ppermute(send_b, "dp", bwd)
            acc_a = got_a.astype(jnp.float32) + left[(2 * n - 2 - t) % n].astype(jnp.float32)
            acc_b = got_b.astype(jnp.float32) + right[(2 + t) % n].astype(jnp.float32)
            if t < n - 2:
                send_a, send_b = acc_a.astype(jnp.bfloat16), acc_b.astype(jnp.bfloat16)
        owned = jnp.concatenate([acc_a, acc_b], axis=1)

        total_sq = all_sum(all_sum(jnp.sum(owned * owned).reshape(1, 1), "dp", n), "mp", blocks)[0, 0]
        clip_factor = jnp.minimum(1.0, math.sqrt(blocks * nseg * seg) / (jnp.sqrt(total_sq) + 1e-06))
        in_use = valid.astype(jnp.float32)[:, None]
        owned_grad = clip_factor * owned
        new_first = in_use * (0.9 * first_moment[0] + 0.1 * owned_grad)
        new_second = in_use * (0.95 * second_moment[0] + 0.05 * owned_grad * owned_grad)
        first_hat = new_first / (1.0 - 0.9**20)
        second_hat = new_second / (1.0 - 0.95**20)
        old_master = master_weights[0]
        new_master = in_use * (
            old_master - 0.02 * (first_hat / (jnp.sqrt(second_hat) + 1e-08) + 0.1 * old_master)
        )
        averaged = 0.9 * average_weights[0] + 0.1 * new_master

        rank_ahead = jnp.array(ring, jnp.int32)[(mypos + jnp.arange(n, dtype=jnp.int32)) % n]
        seg_ahead = (rank_ahead[:, None] * per_rank + jnp.arange(per_rank, dtype=jnp.int32)[None, :]).reshape(-1)
        to_rows = (jnp.arange(cap, dtype=jnp.int32)[:, None] == slot[seg_ahead][None, :]).astype(jnp.bfloat16)
        spread_avg = jnp.dot(to_rows.T, averaged.astype(jnp.bfloat16), preferred_element_type=jnp.bfloat16)
        spread_avg = spread_avg.reshape(n, per_rank, seg)
        avg_l, avg_r = spread_avg[..., :half], spread_avg[..., half:]

        payload = new_master.astype(jnp.bfloat16)
        send_a, send_b = payload[:, :half], payload[:, half:]
        placing_t = placing.T

        def spread(chunk, k):
            return jnp.dot(placing_t[:, k * cap:(k + 1) * cap], chunk, preferred_element_type=jnp.bfloat16)

        out_a = spread(send_a, 0)
        out_b = spread(send_b, 0)
        sum_a = avg_l[n - 1]
        sum_b = avg_r[1]
        for t in range(n - 1):
            send_a = lax.ppermute(send_a, "dp", fwd)
            send_b = lax.ppermute(send_b, "dp", bwd)
            got_a = lax.ppermute(sum_a, "dp", fwd)
            got_b = lax.ppermute(sum_b, "dp", bwd)
            out_a = out_a + spread(send_a, n - 1 - t)
            out_b = out_b + spread(send_b, 1 + t)
            fin_a = got_a.astype(jnp.float32) + avg_l[(2 * n - 2 - t) % n].astype(jnp.float32)
            fin_b = got_b.astype(jnp.float32) + avg_r[(2 + t) % n].astype(jnp.float32)
            if t < n - 2:
                sum_a, sum_b = fin_a.astype(jnp.bfloat16), fin_b.astype(jnp.bfloat16)
        new_params = jnp.concatenate([out_a, out_b], axis=1)
        average_rows = jnp.concatenate([fin_a, fin_b], axis=1)
        return (
            new_params[None],
            new_master[None],
            new_first[None],
            new_second[None],
            average_rows[None],
        )

    return on_device


def solution(mesh):
    return jax.shard_map(
        make_on_device(ring_order(mesh)),
        mesh=mesh,
        in_specs=(
            P("dp", "mp", None, None),
            P(),
            P("mp", "dp", None),
            P("mp", "dp", None),
            P("mp", "dp", None),
            P("mp", "dp", None),
        ),
        out_specs=(
            P("mp", None, None),
            P("mp", "dp", None),
            P("mp", "dp", None),
            P("mp", "dp", None),
            P("mp", "dp", None),
        ),
        check_vma=False,
    )
```

```python
import math

import jax
import jax.numpy as jnp
from jax import lax
from jax.sharding import PartitionSpec as P


def ring_order(mesh):
    n = mesh.shape["dp"]
    try:
        coords = [tuple(mesh.devices[i, 0].coords) for i in range(n)]
        at = {(c[2], c[1]): i for i, c in enumerate(coords)}
        zs = sorted({z for z, _ in at})
        ys = sorted({y for _, y in at})
        if len(at) != n or len(zs) * len(ys) != n:
            return list(range(n))
        if len(ys) % 2:
            if len(zs) % 2:
                return list(range(n))
            at = {(y, z): i for (z, y), i in at.items()}
            zs, ys = ys, zs
        if len(zs) == 1 or len(ys) == 1:
            line = zs if len(ys) == 1 else ys
            return [at[(z, ys[0])] if len(ys) == 1 else at[(zs[0], z)] for z in line]
        cycle = [(z, ys[0]) for z in zs]
        for k, y in enumerate(ys[1:]):
            inner = zs[1:][::-1] if k % 2 == 0 else zs[1:]
            cycle += [(z, y) for z in inner]
        cycle += [(zs[0], y) for y in ys[1:][::-1]]
        return [at[c] for c in cycle]
    except (AttributeError, TypeError, IndexError, KeyError):
        return list(range(n))


def all_sum(v, axis, n):
    if n & (n - 1):
        return lax.psum(v, axis)
    k = 1
    while k < n:
        v = v + lax.ppermute(v, axis, [(i, i ^ k) for i in range(n)])
        k *= 2
    return v


def make_on_device(ring):
    n = len(ring)
    pos_of = [ring.index(r) for r in range(n)]
    fwd = [(ring[q], ring[(q + 1) % n]) for q in range(n)]
    bwd = [(ring[(q + 1) % n], ring[q]) for q in range(n)]

    def on_device(gradients, owner_list, master_weights, first_moment, second_moment, average_weights):
        local_grad = gradients[0, 0]
        nseg, seg = local_grad.shape
        cap = master_weights.shape[1]
        blocks = lax.axis_size("mp")
        per_rank = nseg // n
        half = seg // 2
        me = lax.axis_index("dp")
        mypos = jnp.array(pos_of, jnp.int32)[me]

        warm = jnp.zeros((8, 128), jnp.bfloat16)
        warm = lax.ppermute(warm, "dp", fwd) + lax.ppermute(warm, "dp", bwd)

        position = jnp.arange(nseg, dtype=jnp.int32)
        same_owner = (owner_list[:, None] == owner_list[None, :]) & (position[None, :] < position[:, None])
        within = jnp.sum(same_owner.astype(jnp.int32), axis=1)
        ahead = (jnp.array(pos_of, jnp.int32)[owner_list] - mypos + n) % n
        slot = ahead * cap + within
        hit = jnp.arange(n * cap, dtype=jnp.int32)[:, None] == slot[None, :]
        valid = jnp.any(hit[:cap], axis=1)
        placing = hit.astype(local_grad.dtype)
        left = jnp.dot(placing, local_grad[:, :half], preferred_element_type=jnp.bfloat16).reshape(n, cap, half)
        right = jnp.dot(placing, local_grad[:, half:], preferred_element_type=jnp.bfloat16).reshape(n, cap, half)

        send_a = left[n - 1] + warm[:1, :1]
        send_b = right[1]
        for t in range(n - 1):
            got_a = lax.ppermute(send_a, "dp", fwd)
            got_b = lax.ppermute(send_b, "dp", bwd)
            acc_a = got_a.astype(jnp.float32) + left[(2 * n - 2 - t) % n].astype(jnp.float32)
            acc_b = got_b.astype(jnp.float32) + right[(2 + t) % n].astype(jnp.float32)
            if t < n - 2:
                send_a, send_b = acc_a.astype(jnp.bfloat16), acc_b.astype(jnp.bfloat16)
        owned = jnp.concatenate([acc_a, acc_b], axis=1)

        rank_ahead = jnp.array(ring, jnp.int32)[(mypos + jnp.arange(n, dtype=jnp.int32)) % n]
        seg_ahead = (rank_ahead[:, None] * per_rank + jnp.arange(per_rank, dtype=jnp.int32)[None, :]).reshape(-1)
        to_rows = (jnp.arange(cap, dtype=jnp.int32)[:, None] == slot[seg_ahead][None, :]).astype(jnp.bfloat16)
        spread_avg = jnp.dot(to_rows.T, average_weights[0].astype(jnp.bfloat16), preferred_element_type=jnp.bfloat16)
        spread_avg = spread_avg.reshape(n, per_rank, seg)
        avg_l, avg_r = spread_avg[..., :half], spread_avg[..., half:]
        sum_a, sum_b, owned = lax.optimization_barrier((avg_l[n - 1], avg_r[1], owned))
        for t in range(n - 1):
            got_a = lax.ppermute(sum_a, "dp", fwd)
            got_b = lax.ppermute(sum_b, "dp", bwd)
            fin_a = got_a.astype(jnp.float32) + avg_l[(2 * n - 2 - t) % n].astype(jnp.float32)
            fin_b = got_b.astype(jnp.float32) + avg_r[(2 + t) % n].astype(jnp.float32)
            if t < n - 2:
                sum_a, sum_b = fin_a.astype(jnp.bfloat16), fin_b.astype(jnp.bfloat16)
        old_avg = jnp.concatenate([fin_a, fin_b], axis=1)


        total_sq = all_sum(all_sum(jnp.sum(owned * owned).reshape(1, 1), "dp", n), "mp", blocks)[0, 0]
        clip_factor = jnp.minimum(1.0, math.sqrt(blocks * nseg * seg) / (jnp.sqrt(total_sq) + 1e-06))
        in_use = valid.astype(jnp.float32)[:, None]
        owned_grad = clip_factor * owned
        new_first = in_use * (0.9 * first_moment[0] + 0.1 * owned_grad)
        new_second = in_use * (0.95 * second_moment[0] + 0.05 * owned_grad * owned_grad)
        first_hat = new_first / (1.0 - 0.9**20)
        second_hat = new_second / (1.0 - 0.95**20)
        old_master = master_weights[0]
        new_master = in_use * (
            old_master - 0.02 * (first_hat / (jnp.sqrt(second_hat) + 1e-08) + 0.1 * old_master)
        )

        payload = new_master.astype(jnp.bfloat16)
        send_a, send_b = payload[:, :half], payload[:, half:]
        placing_t = placing.T

        def spread(chunk, k):
            return jnp.dot(placing_t[:, k * cap:(k + 1) * cap], chunk, preferred_element_type=jnp.bfloat16)

        out_a = spread(send_a, 0)
        out_b = spread(send_b, 0)
        for t in range(n - 1):
            send_a = lax.ppermute(send_a, "dp", fwd)
            send_b = lax.ppermute(send_b, "dp", bwd)
            out_a = out_a + spread(send_a, n - 1 - t)
            out_b = out_b + spread(send_b, 1 + t)
        new_params = jnp.concatenate([out_a, out_b], axis=1)
        mine = lax.dynamic_slice_in_dim(new_params, me * per_rank, per_rank, 0).astype(jnp.float32)
        average_rows = 0.9 * old_avg + 0.1 * mine
        return (
            new_params[None],
            new_master[None],
            new_first[None],
            new_second[None],
            average_rows[None],
        )

    return on_device


def solution(mesh):
    return jax.shard_map(
        make_on_device(ring_order(mesh)),
        mesh=mesh,
        in_specs=(
            P("dp", "mp", None, None),
            P(),
            P("mp", "dp", None),
            P("mp", "dp", None),
            P("mp", "dp", None),
            P("mp", "dp", None),
        ),
        out_specs=(
            P("mp", None, None),
            P("mp", "dp", None),
            P("mp", "dp", None),
            P("mp", "dp", None),
            P("mp", "dp", None),
        ),
        check_vma=False,
    )
```

```python
import math

import jax
import jax.numpy as jnp
from jax import lax
from jax.sharding import PartitionSpec as P


def ring_order(mesh):
    n = mesh.shape["dp"]
    try:
        coords = [tuple(mesh.devices[i, 0].coords) for i in range(n)]
        at = {(c[2], c[1]): i for i, c in enumerate(coords)}
        zs = sorted({z for z, _ in at})
        ys = sorted({y for _, y in at})
        if len(at) != n or len(zs) * len(ys) != n:
            return list(range(n))
        if len(ys) % 2:
            if len(zs) % 2:
                return list(range(n))
            at = {(y, z): i for (z, y), i in at.items()}
            zs, ys = ys, zs
        if len(zs) == 1 or len(ys) == 1:
            line = zs if len(ys) == 1 else ys
            return [at[(z, ys[0])] if len(ys) == 1 else at[(zs[0], z)] for z in line]
        cycle = [(z, ys[0]) for z in zs]
        for k, y in enumerate(ys[1:]):
            inner = zs[1:][::-1] if k % 2 == 0 else zs[1:]
            cycle += [(z, y) for z in inner]
        cycle += [(zs[0], y) for y in ys[1:][::-1]]
        return [at[c] for c in cycle]
    except (AttributeError, TypeError, IndexError, KeyError):
        return list(range(n))


def all_sum(v, axis, n):
    if n & (n - 1):
        return lax.psum(v, axis)
    k = 1
    while k < n:
        v = v + lax.ppermute(v, axis, [(i, i ^ k) for i in range(n)])
        k *= 2
    return v


def make_on_device(ring):
    n = len(ring)
    pos_of = [ring.index(r) for r in range(n)]
    fwd = [(ring[q], ring[(q + 1) % n]) for q in range(n)]
    bwd = [(ring[(q + 1) % n], ring[q]) for q in range(n)]

    def on_device(gradients, owner_list, master_weights, first_moment, second_moment, average_weights):
        local_grad = gradients[0, 0]
        nseg, seg = local_grad.shape
        cap = master_weights.shape[1]
        blocks = lax.axis_size("mp")
        per_rank = nseg // n
        half = seg // 2
        me = lax.axis_index("dp")
        mypos = jnp.array(pos_of, jnp.int32)[me]

        warm = jnp.zeros((8, 128), jnp.bfloat16)
        warm = lax.ppermute(warm, "dp", fwd) + lax.ppermute(warm, "dp", bwd)

        position = jnp.arange(nseg, dtype=jnp.int32)
        same_owner = (owner_list[:, None] == owner_list[None, :]) & (position[None, :] < position[:, None])
        within = jnp.sum(same_owner.astype(jnp.int32), axis=1)
        ahead = (jnp.array(pos_of, jnp.int32)[owner_list] - mypos + n) % n
        slot = ahead * cap + within
        hit = jnp.arange(n * cap, dtype=jnp.int32)[:, None] == slot[None, :]
        valid = jnp.any(hit[:cap], axis=1)
        placing = hit.astype(local_grad.dtype)
        left = jnp.dot(placing, local_grad[:, :half], preferred_element_type=jnp.bfloat16).reshape(n, cap, half)
        right = jnp.dot(placing, local_grad[:, half:], preferred_element_type=jnp.bfloat16).reshape(n, cap, half)

        send_a = left[n - 1] + warm[:1, :1]
        send_b = right[1]
        for t in range(n - 1):
            got_a = lax.ppermute(send_a, "dp", fwd)
            got_b = lax.ppermute(send_b, "dp", bwd)
            acc_a = got_a.astype(jnp.float32) + left[(2 * n - 2 - t) % n].astype(jnp.float32)
            acc_b = got_b.astype(jnp.float32) + right[(2 + t) % n].astype(jnp.float32)
            if t < n - 2:
                send_a, send_b = acc_a.astype(jnp.bfloat16), acc_b.astype(jnp.bfloat16)
        owned = jnp.concatenate([acc_a, acc_b], axis=1)

        rank_ahead = jnp.array(ring, jnp.int32)[(mypos + jnp.arange(n, dtype=jnp.int32)) % n]
        seg_ahead = (rank_ahead[:, None] * per_rank + jnp.arange(per_rank, dtype=jnp.int32)[None, :]).reshape(-1)
        to_rows = (jnp.arange(cap, dtype=jnp.int32)[:, None] == slot[seg_ahead][None, :]).astype(jnp.bfloat16)
        spread_avg = jnp.dot(to_rows.T, average_weights[0].astype(jnp.bfloat16), preferred_element_type=jnp.bfloat16)
        spread_avg = spread_avg.reshape(n, per_rank, seg)
        avg_l, avg_r = spread_avg[..., :half], spread_avg[..., half:]
        sum_a, sum_b, owned = lax.optimization_barrier((avg_l[n - 1], avg_r[1], owned))

        def avg_steps(steps, sum_a, sum_b):
            for t in steps:
                got_a = lax.ppermute(sum_a, "dp", fwd)
                got_b = lax.ppermute(sum_b, "dp", bwd)
                fin_a = got_a.astype(jnp.float32) + avg_l[(2 * n - 2 - t) % n].astype(jnp.float32)
                fin_b = got_b.astype(jnp.float32) + avg_r[(2 + t) % n].astype(jnp.float32)
                sum_a, sum_b = fin_a.astype(jnp.bfloat16), fin_b.astype(jnp.bfloat16)
            return sum_a, sum_b, fin_a, fin_b

        early = (n - 1) // 2 + 1
        sum_a, sum_b, _, _ = avg_steps(range(early), sum_a, sum_b)


        total_sq = all_sum(all_sum(jnp.sum(owned * owned).reshape(1, 1), "dp", n), "mp", blocks)[0, 0]
        clip_factor = jnp.minimum(1.0, math.sqrt(blocks * nseg * seg) / (jnp.sqrt(total_sq) + 1e-06))
        in_use = valid.astype(jnp.float32)[:, None]
        owned_grad = clip_factor * owned
        new_first = in_use * (0.9 * first_moment[0] + 0.1 * owned_grad)
        new_second = in_use * (0.95 * second_moment[0] + 0.05 * owned_grad * owned_grad)
        first_hat = new_first / (1.0 - 0.9**20)
        second_hat = new_second / (1.0 - 0.95**20)
        old_master = master_weights[0]
        new_master = in_use * (
            old_master - 0.02 * (first_hat / (jnp.sqrt(second_hat) + 1e-08) + 0.1 * old_master)
        )

        payload, sum_a, sum_b = lax.optimization_barrier((new_master.astype(jnp.bfloat16), sum_a, sum_b))
        _, _, fin_a, fin_b = avg_steps(range(early, n - 1), sum_a, sum_b)
        old_avg = jnp.concatenate([fin_a, fin_b], axis=1)
        send_a, send_b = payload[:, :half], payload[:, half:]
        placing_t = placing.T

        def spread(chunk, k):
            return jnp.dot(placing_t[:, k * cap:(k + 1) * cap], chunk, preferred_element_type=jnp.bfloat16)

        out_a = spread(send_a, 0)
        out_b = spread(send_b, 0)
        for t in range(n - 1):
            send_a = lax.ppermute(send_a, "dp", fwd)
            send_b = lax.ppermute(send_b, "dp", bwd)
            out_a = out_a + spread(send_a, n - 1 - t)
            out_b = out_b + spread(send_b, 1 + t)
        new_params = jnp.concatenate([out_a, out_b], axis=1)
        mine = lax.dynamic_slice_in_dim(new_params, me * per_rank, per_rank, 0).astype(jnp.float32)
        average_rows = 0.9 * old_avg + 0.1 * mine
        return (
            new_params[None],
            new_master[None],
            new_first[None],
            new_second[None],
            average_rows[None],
        )

    return on_device


def solution(mesh):
    return jax.shard_map(
        make_on_device(ring_order(mesh)),
        mesh=mesh,
        in_specs=(
            P("dp", "mp", None, None),
            P(),
            P("mp", "dp", None),
            P("mp", "dp", None),
            P("mp", "dp", None),
            P("mp", "dp", None),
        ),
        out_specs=(
            P("mp", None, None),
            P("mp", "dp", None),
            P("mp", "dp", None),
            P("mp", "dp", None),
            P("mp", "dp", None),
        ),
        check_vma=False,
    )
```

```python
import math

import jax
import jax.numpy as jnp
from jax import lax
from jax.sharding import PartitionSpec as P


def ring_order(mesh):
    n = mesh.shape["dp"]
    try:
        coords = [tuple(mesh.devices[i, 0].coords) for i in range(n)]
        at = {(c[2], c[1]): i for i, c in enumerate(coords)}
        zs = sorted({z for z, _ in at})
        ys = sorted({y for _, y in at})
        if len(at) != n or len(zs) * len(ys) != n:
            return list(range(n))
        if len(ys) % 2:
            if len(zs) % 2:
                return list(range(n))
            at = {(y, z): i for (z, y), i in at.items()}
            zs, ys = ys, zs
        if len(zs) == 1 or len(ys) == 1:
            line = zs if len(ys) == 1 else ys
            return [at[(z, ys[0])] if len(ys) == 1 else at[(zs[0], z)] for z in line]
        cycle = [(z, ys[0]) for z in zs]
        for k, y in enumerate(ys[1:]):
            inner = zs[1:][::-1] if k % 2 == 0 else zs[1:]
            cycle += [(z, y) for z in inner]
        cycle += [(zs[0], y) for y in ys[1:][::-1]]
        return [at[c] for c in cycle]
    except (AttributeError, TypeError, IndexError, KeyError):
        return list(range(n))


def all_sum(v, axis, n):
    if n & (n - 1):
        return lax.psum(v, axis)
    k = 1
    while k < n:
        v = v + lax.ppermute(v, axis, [(i, i ^ k) for i in range(n)])
        k *= 2
    return v


def make_on_device(ring):
    n = len(ring)
    pos_of = [ring.index(r) for r in range(n)]
    fwd = [(ring[q], ring[(q + 1) % n]) for q in range(n)]
    bwd = [(ring[(q + 1) % n], ring[q]) for q in range(n)]

    def on_device(gradients, owner_list, master_weights, first_moment, second_moment, average_weights):
        local_grad = gradients[0, 0]
        nseg, seg = local_grad.shape
        cap = master_weights.shape[1]
        blocks = lax.axis_size("mp")
        per_rank = nseg // n
        half = seg // 2
        me = lax.axis_index("dp")
        mypos = jnp.array(pos_of, jnp.int32)[me]

        warm = jnp.zeros((8, 128), jnp.bfloat16)
        warm = lax.ppermute(warm, "dp", fwd) + lax.ppermute(warm, "dp", bwd)

        position = jnp.arange(nseg, dtype=jnp.int32)
        same_owner = (owner_list[:, None] == owner_list[None, :]) & (position[None, :] < position[:, None])
        within = jnp.sum(same_owner.astype(jnp.int32), axis=1)
        ahead = (jnp.array(pos_of, jnp.int32)[owner_list] - mypos + n) % n
        slot = ahead * cap + within
        hit = jnp.arange(n * cap, dtype=jnp.int32)[:, None] == slot[None, :]
        valid = jnp.any(hit[:cap], axis=1)
        placing = hit.astype(local_grad.dtype)
        left = jnp.dot(placing, local_grad[:, :half], preferred_element_type=jnp.bfloat16).reshape(n, cap, half)
        right = jnp.dot(placing, local_grad[:, half:], preferred_element_type=jnp.bfloat16).reshape(n, cap, half)

        quarter = half // 2
        pieces = (
            (left[..., :quarter], fwd, -1), (right[..., :quarter], bwd, 1),
            (left[..., quarter:], fwd, -1), (right[..., quarter:], bwd, 1),
        )
        sends = [x[(n + d) % n] for x, _, d in pieces]
        sends[0] = sends[0] + warm[:1, :1]
        for t in range(n - 1):
            gots = [lax.ppermute(v, "dp", pairs) for v, (_, pairs, _) in zip(sends, pieces)]
            accs = [
                g.astype(jnp.float32) + x[(2 * n + d * (2 + t)) % n].astype(jnp.float32)
                for g, (x, _, d) in zip(gots, pieces)
            ]
            sends = [a.astype(jnp.bfloat16) for a in accs]
        owned = jnp.concatenate([accs[0], accs[2], accs[1], accs[3]], axis=1)

        total_sq = all_sum(all_sum(jnp.sum(owned * owned).reshape(1, 1), "dp", n), "mp", blocks)[0, 0]
        clip_factor = jnp.minimum(1.0, math.sqrt(blocks * nseg * seg) / (jnp.sqrt(total_sq) + 1e-06))
        in_use = valid.astype(jnp.float32)[:, None]
        owned_grad = clip_factor * owned
        new_first = in_use * (0.9 * first_moment[0] + 0.1 * owned_grad)
        new_second = in_use * (0.95 * second_moment[0] + 0.05 * owned_grad * owned_grad)
        first_hat = new_first / (1.0 - 0.9**20)
        second_hat = new_second / (1.0 - 0.95**20)
        old_master = master_weights[0]
        new_master = in_use * (
            old_master - 0.02 * (first_hat / (jnp.sqrt(second_hat) + 1e-08) + 0.1 * old_master)
        )
        averaged = 0.9 * average_weights[0] + 0.1 * new_master

        rank_ahead = jnp.array(ring, jnp.int32)[(mypos + jnp.arange(n, dtype=jnp.int32)) % n]
        seg_ahead = (rank_ahead[:, None] * per_rank + jnp.arange(per_rank, dtype=jnp.int32)[None, :]).reshape(-1)
        to_rows = (jnp.arange(cap, dtype=jnp.int32)[:, None] == slot[seg_ahead][None, :]).astype(jnp.bfloat16)
        spread_avg = jnp.dot(to_rows.T, averaged.astype(jnp.bfloat16), preferred_element_type=jnp.bfloat16)
        spread_avg = spread_avg.reshape(n, per_rank, seg)
        avg_l, avg_r = spread_avg[..., :half], spread_avg[..., half:]

        payload = new_master.astype(jnp.bfloat16)
        send_a, send_b = payload[:, :half], payload[:, half:]
        placing_t = placing.T

        def spread(chunk, k):
            return jnp.dot(placing_t[:, k * cap:(k + 1) * cap], chunk, preferred_element_type=jnp.bfloat16)

        out_a = spread(send_a, 0)
        out_b = spread(send_b, 0)
        sum_a = avg_l[n - 1]
        sum_b = avg_r[1]
        for t in range(n - 1):
            send_a = lax.ppermute(send_a, "dp", fwd)
            send_b = lax.ppermute(send_b, "dp", bwd)
            got_a = lax.ppermute(sum_a, "dp", fwd)
            got_b = lax.ppermute(sum_b, "dp", bwd)
            out_a = out_a + spread(send_a, n - 1 - t)
            out_b = out_b + spread(send_b, 1 + t)
            fin_a = got_a.astype(jnp.float32) + avg_l[(2 * n - 2 - t) % n].astype(jnp.float32)
            fin_b = got_b.astype(jnp.float32) + avg_r[(2 + t) % n].astype(jnp.float32)
            if t < n - 2:
                sum_a, sum_b = fin_a.astype(jnp.bfloat16), fin_b.astype(jnp.bfloat16)
        new_params = jnp.concatenate([out_a, out_b], axis=1)
        average_rows = jnp.concatenate([fin_a, fin_b], axis=1)
        return (
            new_params[None],
            new_master[None],
            new_first[None],
            new_second[None],
            average_rows[None],
        )

    return on_device


def solution(mesh):
    return jax.shard_map(
        make_on_device(ring_order(mesh)),
        mesh=mesh,
        in_specs=(
            P("dp", "mp", None, None),
            P(),
            P("mp", "dp", None),
            P("mp", "dp", None),
            P("mp", "dp", None),
            P("mp", "dp", None),
        ),
        out_specs=(
            P("mp", None, None),
            P("mp", "dp", None),
            P("mp", "dp", None),
            P("mp", "dp", None),
            P("mp", "dp", None),
        ),
        check_vma=False,
    )
```

```python
import math

import jax
import jax.numpy as jnp
from jax import lax
from jax.sharding import PartitionSpec as P


def ring_order(mesh):
    n = mesh.shape["dp"]
    try:
        coords = [tuple(mesh.devices[i, 0].coords) for i in range(n)]
        at = {(c[2], c[1]): i for i, c in enumerate(coords)}
        zs = sorted({z for z, _ in at})
        ys = sorted({y for _, y in at})
        if len(at) != n or len(zs) * len(ys) != n:
            return list(range(n))
        if len(ys) % 2:
            if len(zs) % 2:
                return list(range(n))
            at = {(y, z): i for (z, y), i in at.items()}
            zs, ys = ys, zs
        if len(zs) == 1 or len(ys) == 1:
            line = zs if len(ys) == 1 else ys
            return [at[(z, ys[0])] if len(ys) == 1 else at[(zs[0], z)] for z in line]
        cycle = [(z, ys[0]) for z in zs]
        for k, y in enumerate(ys[1:]):
            inner = zs[1:][::-1] if k % 2 == 0 else zs[1:]
            cycle += [(z, y) for z in inner]
        cycle += [(zs[0], y) for y in ys[1:][::-1]]
        return [at[c] for c in cycle]
    except (AttributeError, TypeError, IndexError, KeyError):
        return list(range(n))


def all_sum(v, axis, n):
    if n & (n - 1):
        return lax.psum(v, axis)
    k = 1
    while k < n:
        v = v + lax.ppermute(v, axis, [(i, i ^ k) for i in range(n)])
        k *= 2
    return v


def make_on_device(ring):
    n = len(ring)
    pos_of = [ring.index(r) for r in range(n)]
    fwd = [(ring[q], ring[(q + 1) % n]) for q in range(n)]
    bwd = [(ring[(q + 1) % n], ring[q]) for q in range(n)]

    def on_device(gradients, owner_list, master_weights, first_moment, second_moment, average_weights):
        local_grad = gradients[0, 0]
        nseg, seg = local_grad.shape
        cap = master_weights.shape[1]
        blocks = lax.axis_size("mp")
        per_rank = nseg // n
        half = seg // 2
        me = lax.axis_index("dp")
        mypos = jnp.array(pos_of, jnp.int32)[me]

        warm = jnp.zeros((8, 128), jnp.bfloat16)
        warm = lax.ppermute(warm, "dp", fwd) + lax.ppermute(warm, "dp", bwd)

        position = jnp.arange(nseg, dtype=jnp.int32)
        same_owner = (owner_list[:, None] == owner_list[None, :]) & (position[None, :] < position[:, None])
        within = jnp.sum(same_owner.astype(jnp.int32), axis=1)
        ahead = (jnp.array(pos_of, jnp.int32)[owner_list] - mypos + n) % n
        slot = ahead * cap + within
        hit = jnp.arange(n * cap, dtype=jnp.int32)[:, None] == slot[None, :]
        valid = jnp.any(hit[:cap], axis=1)
        placing = hit.astype(local_grad.dtype)
        left = jnp.dot(placing, local_grad[:, :half], preferred_element_type=jnp.bfloat16).reshape(n, cap, half)
        right = jnp.dot(placing, local_grad[:, half:], preferred_element_type=jnp.bfloat16).reshape(n, cap, half)

        send_a = left[n - 1] + warm[:1, :1]
        send_b = right[1]
        for t in range(n - 1):
            got_a = lax.ppermute(send_a, "dp", fwd)
            got_b = lax.ppermute(send_b, "dp", bwd)
            acc_a = got_a.astype(jnp.float32) + left[(2 * n - 2 - t) % n].astype(jnp.float32)
            acc_b = got_b.astype(jnp.float32) + right[(2 + t) % n].astype(jnp.float32)
            if t < n - 2:
                send_a, send_b = acc_a.astype(jnp.bfloat16), acc_b.astype(jnp.bfloat16)
        owned = jnp.concatenate([acc_a, acc_b], axis=1)

        rank_ahead = jnp.array(ring, jnp.int32)[(mypos + jnp.arange(n, dtype=jnp.int32)) % n]
        seg_ahead = (rank_ahead[:, None] * per_rank + jnp.arange(per_rank, dtype=jnp.int32)[None, :]).reshape(-1)
        to_rows = (jnp.arange(cap, dtype=jnp.int32)[:, None] == slot[seg_ahead][None, :]).astype(jnp.bfloat16)
        spread_avg = jnp.dot(to_rows.T, average_weights[0].astype(jnp.bfloat16), preferred_element_type=jnp.bfloat16)
        spread_avg = spread_avg.reshape(n, per_rank, seg)
        avg_l, avg_r = spread_avg[..., :half], spread_avg[..., half:]

        def avg_steps(steps, sum_a, sum_b):
            fin_a = fin_b = None
            for t in steps:
                got_a = lax.ppermute(sum_a, "dp", fwd)
                got_b = lax.ppermute(sum_b, "dp", bwd)
                fin_a = got_a.astype(jnp.float32) + avg_l[(2 * n - 2 - t) % n].astype(jnp.float32)
                fin_b = got_b.astype(jnp.float32) + avg_r[(2 + t) % n].astype(jnp.float32)
                sum_a, sum_b = fin_a.astype(jnp.bfloat16), fin_b.astype(jnp.bfloat16)
            return sum_a, sum_b, fin_a, fin_b

        total_sq = all_sum(all_sum(jnp.sum(owned * owned).reshape(1, 1), "dp", n), "mp", blocks)[0, 0]
        clip_factor = jnp.minimum(1.0, math.sqrt(blocks * nseg * seg) / (jnp.sqrt(total_sq) + 1e-06))
        sum_a, sum_b, clip_factor = lax.optimization_barrier((avg_l[n - 1], avg_r[1], clip_factor))
        early = 2 if n > 3 else 0
        sum_a, sum_b, _, _ = avg_steps(range(early), sum_a, sum_b)
        in_use = valid.astype(jnp.float32)[:, None]
        owned_grad = clip_factor * owned
        new_first = in_use * (0.9 * first_moment[0] + 0.1 * owned_grad)
        new_second = in_use * (0.95 * second_moment[0] + 0.05 * owned_grad * owned_grad)
        first_hat = new_first / (1.0 - 0.9**20)
        second_hat = new_second / (1.0 - 0.95**20)
        old_master = master_weights[0]
        new_master = in_use * (
            old_master - 0.02 * (first_hat / (jnp.sqrt(second_hat) + 1e-08) + 0.1 * old_master)
        )

        payload, sum_a, sum_b = lax.optimization_barrier((new_master.astype(jnp.bfloat16), sum_a, sum_b))
        _, _, fin_a, fin_b = avg_steps(range(early, n - 1), sum_a, sum_b)
        old_avg = jnp.concatenate([fin_a, fin_b], axis=1)
        send_a, send_b = payload[:, :half], payload[:, half:]
        placing_t = placing.T

        def spread(chunk, k):
            return jnp.dot(placing_t[:, k * cap:(k + 1) * cap], chunk, preferred_element_type=jnp.bfloat16)

        out_a = spread(send_a, 0)
        out_b = spread(send_b, 0)
        for t in range(n - 1):
            send_a = lax.ppermute(send_a, "dp", fwd)
            send_b = lax.ppermute(send_b, "dp", bwd)
            out_a = out_a + spread(send_a, n - 1 - t)
            out_b = out_b + spread(send_b, 1 + t)
        new_params = jnp.concatenate([out_a, out_b], axis=1)
        mine = lax.dynamic_slice_in_dim(new_params, me * per_rank, per_rank, 0).astype(jnp.float32)
        average_rows = 0.9 * old_avg + 0.1 * mine
        return (
            new_params[None],
            new_master[None],
            new_first[None],
            new_second[None],
            average_rows[None],
        )

    return on_device


def solution(mesh):
    return jax.shard_map(
        make_on_device(ring_order(mesh)),
        mesh=mesh,
        in_specs=(
            P("dp", "mp", None, None),
            P(),
            P("mp", "dp", None),
            P("mp", "dp", None),
            P("mp", "dp", None),
            P("mp", "dp", None),
        ),
        out_specs=(
            P("mp", None, None),
            P("mp", "dp", None),
            P("mp", "dp", None),
            P("mp", "dp", None),
            P("mp", "dp", None),
        ),
        check_vma=False,
    )
```

```python
import math

import jax
import jax.numpy as jnp
from jax import lax
from jax.sharding import PartitionSpec as P


def ring_order(mesh):
    n = mesh.shape["dp"]
    try:
        coords = [tuple(mesh.devices[i, 0].coords) for i in range(n)]
        at = {(c[2], c[1]): i for i, c in enumerate(coords)}
        zs = sorted({z for z, _ in at})
        ys = sorted({y for _, y in at})
        if len(at) != n or len(zs) * len(ys) != n:
            return list(range(n))
        if len(ys) % 2:
            if len(zs) % 2:
                return list(range(n))
            at = {(y, z): i for (z, y), i in at.items()}
            zs, ys = ys, zs
        if len(zs) == 1 or len(ys) == 1:
            line = zs if len(ys) == 1 else ys
            return [at[(z, ys[0])] if len(ys) == 1 else at[(zs[0], z)] for z in line]
        cycle = [(z, ys[0]) for z in zs]
        for k, y in enumerate(ys[1:]):
            inner = zs[1:][::-1] if k % 2 == 0 else zs[1:]
            cycle += [(z, y) for z in inner]
        cycle += [(zs[0], y) for y in ys[1:][::-1]]
        return [at[c] for c in cycle]
    except (AttributeError, TypeError, IndexError, KeyError):
        return list(range(n))


def all_sum(v, axis, n):
    if n & (n - 1):
        return lax.psum(v, axis)
    k = 1
    while k < n:
        v = v + lax.ppermute(v, axis, [(i, i ^ k) for i in range(n)])
        k *= 2
    return v


def make_on_device(ring):
    n = len(ring)
    pos_of = [ring.index(r) for r in range(n)]
    fwd = [(ring[q], ring[(q + 1) % n]) for q in range(n)]
    bwd = [(ring[(q + 1) % n], ring[q]) for q in range(n)]

    def on_device(gradients, owner_list, master_weights, first_moment, second_moment, average_weights):
        local_grad = gradients[0, 0]
        nseg, seg = local_grad.shape
        cap = master_weights.shape[1]
        blocks = lax.axis_size("mp")
        per_rank = nseg // n
        half = seg // 2
        me = lax.axis_index("dp")
        mypos = jnp.array(pos_of, jnp.int32)[me]

        warm = jnp.zeros((8, 128), jnp.bfloat16)
        warm = lax.ppermute(warm, "dp", fwd) + lax.ppermute(warm, "dp", bwd)

        position = jnp.arange(nseg, dtype=jnp.int32)
        same_owner = (owner_list[:, None] == owner_list[None, :]) & (position[None, :] < position[:, None])
        within = jnp.sum(same_owner.astype(jnp.int32), axis=1)
        ahead = (jnp.array(pos_of, jnp.int32)[owner_list] - mypos + n) % n
        slot = ahead * cap + within
        hit = jnp.arange(n * cap, dtype=jnp.int32)[:, None] == slot[None, :]
        valid = jnp.any(hit[:cap], axis=1)
        placing = hit.astype(local_grad.dtype)
        left = jnp.dot(placing, local_grad[:, :half], preferred_element_type=jnp.bfloat16).reshape(n, cap, half)
        right = jnp.dot(placing, local_grad[:, half:], preferred_element_type=jnp.bfloat16).reshape(n, cap, half)

        send_a = left[n - 1] + warm[:1, :1]
        send_b = right[1]
        for t in range(n - 1):
            got_a = lax.ppermute(send_a, "dp", fwd)
            got_b = lax.ppermute(send_b, "dp", bwd)
            acc_a = got_a.astype(jnp.float32) + left[(2 * n - 2 - t) % n].astype(jnp.float32)
            acc_b = got_b.astype(jnp.float32) + right[(2 + t) % n].astype(jnp.float32)
            if t < n - 2:
                send_a, send_b = acc_a.astype(jnp.bfloat16), acc_b.astype(jnp.bfloat16)
        owned = jnp.concatenate([acc_a, acc_b], axis=1)

        to_rows = (jnp.arange(cap, dtype=jnp.int32)[:, None] == slot[None, :]).astype(jnp.bfloat16)
        spread_avg = jnp.dot(to_rows.T, average_weights[0].astype(jnp.bfloat16), preferred_element_type=jnp.bfloat16)
        old_avg = lax.psum_scatter(spread_avg, "dp", scatter_dimension=0, tiled=True).astype(jnp.float32)


        total_sq = all_sum(all_sum(jnp.sum(owned * owned).reshape(1, 1), "dp", n), "mp", blocks)[0, 0]
        clip_factor = jnp.minimum(1.0, math.sqrt(blocks * nseg * seg) / (jnp.sqrt(total_sq) + 1e-06))
        in_use = valid.astype(jnp.float32)[:, None]
        owned_grad = clip_factor * owned
        new_first = in_use * (0.9 * first_moment[0] + 0.1 * owned_grad)
        new_second = in_use * (0.95 * second_moment[0] + 0.05 * owned_grad * owned_grad)
        first_hat = new_first / (1.0 - 0.9**20)
        second_hat = new_second / (1.0 - 0.95**20)
        old_master = master_weights[0]
        new_master = in_use * (
            old_master - 0.02 * (first_hat / (jnp.sqrt(second_hat) + 1e-08) + 0.1 * old_master)
        )

        payload = new_master.astype(jnp.bfloat16)
        send_a, send_b = payload[:, :half], payload[:, half:]
        placing_t = placing.T

        def spread(chunk, k):
            return jnp.dot(placing_t[:, k * cap:(k + 1) * cap], chunk, preferred_element_type=jnp.bfloat16)

        out_a = spread(send_a, 0)
        out_b = spread(send_b, 0)
        for t in range(n - 1):
            send_a = lax.ppermute(send_a, "dp", fwd)
            send_b = lax.ppermute(send_b, "dp", bwd)
            out_a = out_a + spread(send_a, n - 1 - t)
            out_b = out_b + spread(send_b, 1 + t)
        new_params = jnp.concatenate([out_a, out_b], axis=1)
        mine = lax.dynamic_slice_in_dim(new_params, me * per_rank, per_rank, 0).astype(jnp.float32)
        average_rows = 0.9 * old_avg + 0.1 * mine
        return (
            new_params[None],
            new_master[None],
            new_first[None],
            new_second[None],
            average_rows[None],
        )

    return on_device


def solution(mesh):
    return jax.shard_map(
        make_on_device(ring_order(mesh)),
        mesh=mesh,
        in_specs=(
            P("dp", "mp", None, None),
            P(),
            P("mp", "dp", None),
            P("mp", "dp", None),
            P("mp", "dp", None),
            P("mp", "dp", None),
        ),
        out_specs=(
            P("mp", None, None),
            P("mp", "dp", None),
            P("mp", "dp", None),
            P("mp", "dp", None),
            P("mp", "dp", None),
        ),
        check_vma=False,
    )
```

```python
import math

import jax
import jax.numpy as jnp
from jax import lax
from jax.sharding import PartitionSpec as P


def ring_order(mesh):
    n = mesh.shape["dp"]
    try:
        coords = [tuple(mesh.devices[i, 0].coords) for i in range(n)]
        at = {(c[2], c[1]): i for i, c in enumerate(coords)}
        zs = sorted({z for z, _ in at})
        ys = sorted({y for _, y in at})
        if len(at) != n or len(zs) * len(ys) != n:
            return list(range(n))
        if len(ys) % 2:
            if len(zs) % 2:
                return list(range(n))
            at = {(y, z): i for (z, y), i in at.items()}
            zs, ys = ys, zs
        if len(zs) == 1 or len(ys) == 1:
            line = zs if len(ys) == 1 else ys
            return [at[(z, ys[0])] if len(ys) == 1 else at[(zs[0], z)] for z in line]
        cycle = [(z, ys[0]) for z in zs]
        for k, y in enumerate(ys[1:]):
            inner = zs[1:][::-1] if k % 2 == 0 else zs[1:]
            cycle += [(z, y) for z in inner]
        cycle += [(zs[0], y) for y in ys[1:][::-1]]
        return [at[c] for c in cycle]
    except (AttributeError, TypeError, IndexError, KeyError):
        return list(range(n))


def all_sum(v, axis, n):
    if n & (n - 1):
        return lax.psum(v, axis)
    k = 1
    while k < n:
        v = v + lax.ppermute(v, axis, [(i, i ^ k) for i in range(n)])
        k *= 2
    return v


def make_on_device(ring):
    n = len(ring)
    pos_of = [ring.index(r) for r in range(n)]
    fwd = [(ring[q], ring[(q + 1) % n]) for q in range(n)]
    bwd = [(ring[(q + 1) % n], ring[q]) for q in range(n)]

    def on_device(gradients, owner_list, master_weights, first_moment, second_moment, average_weights):
        local_grad = gradients[0, 0]
        nseg, seg = local_grad.shape
        cap = master_weights.shape[1]
        blocks = lax.axis_size("mp")
        per_rank = nseg // n
        half = seg // 2
        me = lax.axis_index("dp")
        mypos = jnp.array(pos_of, jnp.int32)[me]

        warm = jnp.zeros((8, 128), jnp.bfloat16)
        warm = lax.ppermute(warm, "dp", fwd) + lax.ppermute(warm, "dp", bwd)

        position = jnp.arange(nseg, dtype=jnp.int32)
        same_owner = (owner_list[:, None] == owner_list[None, :]) & (position[None, :] < position[:, None])
        within = jnp.sum(same_owner.astype(jnp.int32), axis=1)
        ahead = (jnp.array(pos_of, jnp.int32)[owner_list] - mypos + n) % n
        slot = ahead * cap + within
        hit = jnp.arange(n * cap, dtype=jnp.int32)[:, None] == slot[None, :]
        valid = jnp.any(hit[:cap], axis=1)
        placing = hit.astype(local_grad.dtype)
        left = jnp.dot(placing, local_grad[:, :half], preferred_element_type=jnp.bfloat16).reshape(n, cap, half)
        right = jnp.dot(placing, local_grad[:, half:], preferred_element_type=jnp.bfloat16).reshape(n, cap, half)

        send_a = left[n - 1] + warm[:1, :1]
        send_b = right[1]
        for t in range(n - 1):
            got_a = lax.ppermute(send_a, "dp", fwd)
            got_b = lax.ppermute(send_b, "dp", bwd)
            acc_a = got_a.astype(jnp.float32) + left[(2 * n - 2 - t) % n].astype(jnp.float32)
            acc_b = got_b.astype(jnp.float32) + right[(2 + t) % n].astype(jnp.float32)
            if t < n - 2:
                send_a, send_b = acc_a.astype(jnp.bfloat16), acc_b.astype(jnp.bfloat16)
        owned = jnp.concatenate([acc_a, acc_b], axis=1)

        total_sq = all_sum(all_sum(jnp.sum(owned * owned).reshape(1, 1), "dp", n), "mp", blocks)[0, 0]
        clip_factor = jnp.minimum(1.0, math.sqrt(blocks * nseg * seg) / (jnp.sqrt(total_sq) + 1e-06))
        in_use = valid.astype(jnp.float32)[:, None]
        owned_grad = clip_factor * owned
        new_first = in_use * (0.9 * first_moment[0] + 0.1 * owned_grad)
        new_second = in_use * (0.95 * second_moment[0] + 0.05 * owned_grad * owned_grad)
        first_hat = new_first / (1.0 - 0.9**20)
        second_hat = new_second / (1.0 - 0.95**20)
        old_master = master_weights[0]
        new_master = in_use * (
            old_master - 0.02 * (first_hat / (jnp.sqrt(second_hat) + 1e-08) + 0.1 * old_master)
        )
        averaged = 0.9 * average_weights[0] + 0.1 * new_master

        rank_ahead = jnp.array(ring, jnp.int32)[(mypos + jnp.arange(n, dtype=jnp.int32)) % n]
        seg_ahead = (rank_ahead[:, None] * per_rank + jnp.arange(per_rank, dtype=jnp.int32)[None, :]).reshape(-1)
        to_rows = (jnp.arange(cap, dtype=jnp.int32)[:, None] == slot[seg_ahead][None, :]).astype(jnp.bfloat16)
        spread_avg = jnp.dot(to_rows.T, averaged.astype(jnp.bfloat16), preferred_element_type=jnp.bfloat16)
        spread_avg = spread_avg.reshape(n, per_rank, seg)
        avg_l, avg_r = spread_avg[..., :half], spread_avg[..., half:]

        payload = new_master.astype(jnp.bfloat16)
        send_a, send_b = payload[:, :half], payload[:, half:]
        placing_t = placing.T

        def spread(chunk, k):
            return jnp.dot(placing_t[:, k * cap:(k + 1) * cap], chunk, preferred_element_type=jnp.bfloat16)

        out_a = spread(send_a, 0)
        out_b = spread(send_b, 0)
        sum_a = avg_l[n - 1]
        sum_b = avg_r[1]
        for t in range(n - 1):
            both_a = lax.ppermute(jnp.concatenate([send_a, sum_a], axis=0), "dp", fwd)
            both_b = lax.ppermute(jnp.concatenate([send_b, sum_b], axis=0), "dp", bwd)
            send_a, got_a = both_a[:cap], both_a[cap:]
            send_b, got_b = both_b[:cap], both_b[cap:]
            out_a = out_a + spread(send_a, n - 1 - t)
            out_b = out_b + spread(send_b, 1 + t)
            fin_a = got_a.astype(jnp.float32) + avg_l[(2 * n - 2 - t) % n].astype(jnp.float32)
            fin_b = got_b.astype(jnp.float32) + avg_r[(2 + t) % n].astype(jnp.float32)
            if t < n - 2:
                sum_a, sum_b = fin_a.astype(jnp.bfloat16), fin_b.astype(jnp.bfloat16)
        new_params = jnp.concatenate([out_a, out_b], axis=1)
        average_rows = jnp.concatenate([fin_a, fin_b], axis=1)
        return (
            new_params[None],
            new_master[None],
            new_first[None],
            new_second[None],
            average_rows[None],
        )

    return on_device


def solution(mesh):
    return jax.shard_map(
        make_on_device(ring_order(mesh)),
        mesh=mesh,
        in_specs=(
            P("dp", "mp", None, None),
            P(),
            P("mp", "dp", None),
            P("mp", "dp", None),
            P("mp", "dp", None),
            P("mp", "dp", None),
        ),
        out_specs=(
            P("mp", None, None),
            P("mp", "dp", None),
            P("mp", "dp", None),
            P("mp", "dp", None),
            P("mp", "dp", None),
        ),
        check_vma=False,
    )
```

```python
import math

import jax
import jax.numpy as jnp
from jax import lax
from jax.sharding import PartitionSpec as P


def ring_order(mesh):
    n = mesh.shape["dp"]
    try:
        coords = [tuple(mesh.devices[i, 0].coords) for i in range(n)]
        at = {(c[2], c[1]): i for i, c in enumerate(coords)}
        zs = sorted({z for z, _ in at})
        ys = sorted({y for _, y in at})
        if len(at) != n or len(zs) * len(ys) != n:
            return list(range(n))
        if len(ys) % 2:
            if len(zs) % 2:
                return list(range(n))
            at = {(y, z): i for (z, y), i in at.items()}
            zs, ys = ys, zs
        if len(zs) == 1 or len(ys) == 1:
            line = zs if len(ys) == 1 else ys
            return [at[(z, ys[0])] if len(ys) == 1 else at[(zs[0], z)] for z in line]
        cycle = [(z, ys[0]) for z in zs]
        for k, y in enumerate(ys[1:]):
            inner = zs[1:][::-1] if k % 2 == 0 else zs[1:]
            cycle += [(z, y) for z in inner]
        cycle += [(zs[0], y) for y in ys[1:][::-1]]
        return [at[c] for c in cycle]
    except (AttributeError, TypeError, IndexError, KeyError):
        return list(range(n))


def all_sum(v, axis, n):
    if n & (n - 1):
        return lax.psum(v, axis)
    k = 1
    while k < n:
        v = v + lax.ppermute(v, axis, [(i, i ^ k) for i in range(n)])
        k *= 2
    return v


def make_on_device(ring):
    n = len(ring)
    pos_of = [ring.index(r) for r in range(n)]
    fwd = [(ring[q], ring[(q + 1) % n]) for q in range(n)]
    bwd = [(ring[(q + 1) % n], ring[q]) for q in range(n)]

    def on_device(gradients, owner_list, master_weights, first_moment, second_moment, average_weights):
        local_grad = gradients[0, 0]
        nseg, seg = local_grad.shape
        cap = master_weights.shape[1]
        blocks = lax.axis_size("mp")
        per_rank = nseg // n
        half = seg // 2
        me = lax.axis_index("dp")
        mypos = jnp.array(pos_of, jnp.int32)[me]

        warm = jnp.zeros((8, 128), jnp.bfloat16)
        warm = lax.ppermute(warm, "dp", fwd) + lax.ppermute(warm, "dp", bwd)

        position = jnp.arange(nseg, dtype=jnp.int32)
        same_owner = (owner_list[:, None] == owner_list[None, :]) & (position[None, :] < position[:, None])
        within = jnp.sum(same_owner.astype(jnp.int32), axis=1)
        ahead = (jnp.array(pos_of, jnp.int32)[owner_list] - mypos + n) % n
        slot = ahead * cap + within
        hit = jnp.arange(n * cap, dtype=jnp.int32)[:, None] == slot[None, :]
        valid = jnp.any(hit[:cap], axis=1)
        placing = hit.astype(local_grad.dtype)
        left = jnp.dot(placing, local_grad[:, :half], preferred_element_type=jnp.bfloat16).reshape(n, cap, half)
        right = jnp.dot(placing, local_grad[:, half:], preferred_element_type=jnp.bfloat16).reshape(n, cap, half)

        send_a = left[n - 1] + warm[:1, :1]
        send_b = right[1]
        for t in range(n - 1):
            got_a = lax.ppermute(send_a, "dp", fwd)
            got_b = lax.ppermute(send_b, "dp", bwd)
            acc_a = got_a.astype(jnp.float32) + left[(2 * n - 2 - t) % n].astype(jnp.float32)
            acc_b = got_b.astype(jnp.float32) + right[(2 + t) % n].astype(jnp.float32)
            if t < n - 2:
                send_a, send_b = acc_a.astype(jnp.bfloat16), acc_b.astype(jnp.bfloat16)
        owned = jnp.concatenate([acc_a, acc_b], axis=1)

        total_sq = all_sum(all_sum(jnp.sum(owned * owned).reshape(1, 1), "dp", n), "mp", blocks)[0, 0]
        clip_factor = jnp.minimum(1.0, math.sqrt(blocks * nseg * seg) / (jnp.sqrt(total_sq) + 1e-06))
        in_use = valid.astype(jnp.float32)[:, None]
        owned_grad = clip_factor * owned
        new_first = in_use * (0.9 * first_moment[0] + 0.1 * owned_grad)
        new_second = in_use * (0.95 * second_moment[0] + 0.05 * owned_grad * owned_grad)
        first_hat = new_first / (1.0 - 0.9**20)
        second_hat = new_second / (1.0 - 0.95**20)
        old_master = master_weights[0]
        new_master = in_use * (
            old_master - 0.02 * (first_hat / (jnp.sqrt(second_hat) + 1e-08) + 0.1 * old_master)
        )
        averaged = 0.9 * average_weights[0] + 0.1 * new_master

        rank_ahead = jnp.array(ring, jnp.int32)[(mypos + jnp.arange(n, dtype=jnp.int32)) % n]
        seg_ahead = (rank_ahead[:, None] * per_rank + jnp.arange(per_rank, dtype=jnp.int32)[None, :]).reshape(-1)
        to_rows = (jnp.arange(cap, dtype=jnp.int32)[:, None] == slot[seg_ahead][None, :]).astype(jnp.bfloat16)
        spread_avg = jnp.dot(to_rows.T, averaged.astype(jnp.bfloat16), preferred_element_type=jnp.bfloat16)
        spread_avg = spread_avg.reshape(n, per_rank, seg)
        avg_l, avg_r = spread_avg[..., :half], spread_avg[..., half:]

        payload = new_master.astype(jnp.bfloat16)
        send_a, send_b = payload[:, :half], payload[:, half:]
        placing_t = placing.T

        def spread(chunk, k):
            return jnp.dot(placing_t[:, k * cap:(k + 1) * cap], chunk, preferred_element_type=jnp.bfloat16)

        out_a = spread(send_a, 0)
        out_b = spread(send_b, 0)
        sum_a = avg_l[n - 1]
        sum_b = avg_r[1]
        for t in range(n - 1):
            send_a = lax.ppermute(send_a, "dp", fwd)
            send_b = lax.ppermute(send_b, "dp", bwd)
            got_a = lax.ppermute(sum_a, "dp", fwd)
            got_b = lax.ppermute(sum_b, "dp", bwd)
            if t == 0:
                new_master, new_first, new_second, send_a, send_b = lax.optimization_barrier(
                    (new_master, new_first, new_second, send_a, send_b)
                )
            out_a = out_a + spread(send_a, n - 1 - t)
            out_b = out_b + spread(send_b, 1 + t)
            fin_a = got_a.astype(jnp.float32) + avg_l[(2 * n - 2 - t) % n].astype(jnp.float32)
            fin_b = got_b.astype(jnp.float32) + avg_r[(2 + t) % n].astype(jnp.float32)
            if t < n - 2:
                sum_a, sum_b = fin_a.astype(jnp.bfloat16), fin_b.astype(jnp.bfloat16)
        new_params = jnp.concatenate([out_a, out_b], axis=1)
        average_rows = jnp.concatenate([fin_a, fin_b], axis=1)
        return (
            new_params[None],
            new_master[None],
            new_first[None],
            new_second[None],
            average_rows[None],
        )

    return on_device


def solution(mesh):
    return jax.shard_map(
        make_on_device(ring_order(mesh)),
        mesh=mesh,
        in_specs=(
            P("dp", "mp", None, None),
            P(),
            P("mp", "dp", None),
            P("mp", "dp", None),
            P("mp", "dp", None),
            P("mp", "dp", None),
        ),
        out_specs=(
            P("mp", None, None),
            P("mp", "dp", None),
            P("mp", "dp", None),
            P("mp", "dp", None),
            P("mp", "dp", None),
        ),
        check_vma=False,
    )
```

```python
import math

import jax
import jax.numpy as jnp
from jax import lax
from jax.sharding import PartitionSpec as P


def ring_order(mesh):
    n = mesh.shape["dp"]
    try:
        coords = [tuple(mesh.devices[i, 0].coords) for i in range(n)]
        at = {(c[2], c[1]): i for i, c in enumerate(coords)}
        zs = sorted({z for z, _ in at})
        ys = sorted({y for _, y in at})
        if len(at) != n or len(zs) * len(ys) != n:
            return list(range(n))
        if len(ys) % 2:
            if len(zs) % 2:
                return list(range(n))
            at = {(y, z): i for (z, y), i in at.items()}
            zs, ys = ys, zs
        if len(zs) == 1 or len(ys) == 1:
            line = zs if len(ys) == 1 else ys
            return [at[(z, ys[0])] if len(ys) == 1 else at[(zs[0], z)] for z in line]
        cycle = [(z, ys[0]) for z in zs]
        for k, y in enumerate(ys[1:]):
            inner = zs[1:][::-1] if k % 2 == 0 else zs[1:]
            cycle += [(z, y) for z in inner]
        cycle += [(zs[0], y) for y in ys[1:][::-1]]
        return [at[c] for c in cycle]
    except (AttributeError, TypeError, IndexError, KeyError):
        return list(range(n))


def all_sum(v, axis, n):
    if n & (n - 1):
        return lax.psum(v, axis)
    k = 1
    while k < n:
        v = v + lax.ppermute(v, axis, [(i, i ^ k) for i in range(n)])
        k *= 2
    return v


def make_on_device(ring):
    n = len(ring)
    pos_of = [ring.index(r) for r in range(n)]
    fwd = [(ring[q], ring[(q + 1) % n]) for q in range(n)]
    bwd = [(ring[(q + 1) % n], ring[q]) for q in range(n)]

    def on_device(gradients, owner_list, master_weights, first_moment, second_moment, average_weights):
        local_grad = gradients[0, 0]
        nseg, seg = local_grad.shape
        cap = master_weights.shape[1]
        blocks = lax.axis_size("mp")
        per_rank = nseg // n
        half = seg // 2
        me = lax.axis_index("dp")
        mypos = jnp.array(pos_of, jnp.int32)[me]

        warm = jnp.zeros((8, 128), jnp.bfloat16)
        warm = lax.ppermute(warm, "dp", fwd) + lax.ppermute(warm, "dp", bwd)

        position = jnp.arange(nseg, dtype=jnp.int32)
        same_owner = (owner_list[:, None] == owner_list[None, :]) & (position[None, :] < position[:, None])
        within = jnp.sum(same_owner.astype(jnp.int32), axis=1)
        ahead = (jnp.array(pos_of, jnp.int32)[owner_list] - mypos + n) % n
        slot = ahead * cap + within
        hit = jnp.arange(n * cap, dtype=jnp.int32)[:, None] == slot[None, :]
        valid = jnp.any(hit[:cap], axis=1)
        placing = hit.astype(local_grad.dtype)
        left = jnp.dot(placing, local_grad[:, :half], preferred_element_type=jnp.bfloat16).reshape(n, cap, half)
        right = jnp.dot(placing, local_grad[:, half:], preferred_element_type=jnp.bfloat16).reshape(n, cap, half)

        send_a = left[n - 1] + warm[:1, :1]
        send_b = right[1]
        for t in range(n - 1):
            got_a = lax.ppermute(send_a, "dp", fwd)
            got_b = lax.ppermute(send_b, "dp", bwd)
            acc_a = got_a.astype(jnp.float32) + left[(2 * n - 2 - t) % n].astype(jnp.float32)
            acc_b = got_b.astype(jnp.float32) + right[(2 + t) % n].astype(jnp.float32)
            if t < n - 2:
                send_a, send_b = acc_a.astype(jnp.bfloat16), acc_b.astype(jnp.bfloat16)
        total_sq = all_sum(all_sum((jnp.sum(acc_a * acc_a) + jnp.sum(acc_b * acc_b)).reshape(1, 1), "dp", n), "mp", blocks)[0, 0]
        clip_factor = jnp.minimum(1.0, math.sqrt(blocks * nseg * seg) / (jnp.sqrt(total_sq) + 1e-06))
        in_use = valid.astype(jnp.float32)[:, None]

        def update(cols, grad):
            owned_grad = clip_factor * grad
            new_first = in_use * (0.9 * first_moment[0][:, cols] + 0.1 * owned_grad)
            new_second = in_use * (0.95 * second_moment[0][:, cols] + 0.05 * owned_grad * owned_grad)
            first_hat = new_first / (1.0 - 0.9**20)
            second_hat = new_second / (1.0 - 0.95**20)
            old_master = master_weights[0][:, cols]
            new_master = in_use * (
                old_master - 0.02 * (first_hat / (jnp.sqrt(second_hat) + 1e-08) + 0.1 * old_master)
            )
            averaged = 0.9 * average_weights[0][:, cols] + 0.1 * new_master
            return new_first, new_second, new_master, averaged

        upd_a = update(slice(0, half), acc_a)
        upd_b = update(slice(half, seg), acc_b)
        new_first, new_second, new_master = (jnp.concatenate([x, y], axis=1) for x, y in zip(upd_a[:3], upd_b[:3]))

        rank_ahead = jnp.array(ring, jnp.int32)[(mypos + jnp.arange(n, dtype=jnp.int32)) % n]
        seg_ahead = (rank_ahead[:, None] * per_rank + jnp.arange(per_rank, dtype=jnp.int32)[None, :]).reshape(-1)
        to_rows = (jnp.arange(cap, dtype=jnp.int32)[:, None] == slot[seg_ahead][None, :]).astype(jnp.bfloat16)
        avg_l, avg_r = (
            jnp.dot(to_rows.T, u[3].astype(jnp.bfloat16), preferred_element_type=jnp.bfloat16).reshape(n, per_rank, half)
            for u in (upd_a, upd_b)
        )
        send_a, send_b = upd_a[2].astype(jnp.bfloat16), upd_b[2].astype(jnp.bfloat16)
        placing_t = placing.T

        def spread(chunk, k):
            return jnp.dot(placing_t[:, k * cap:(k + 1) * cap], chunk, preferred_element_type=jnp.bfloat16)

        out_a = spread(send_a, 0)
        out_b = spread(send_b, 0)
        sum_a = avg_l[n - 1]
        sum_b = avg_r[1]
        for t in range(n - 1):
            send_a = lax.ppermute(send_a, "dp", fwd)
            send_b = lax.ppermute(send_b, "dp", bwd)
            got_a = lax.ppermute(sum_a, "dp", fwd)
            got_b = lax.ppermute(sum_b, "dp", bwd)
            out_a = out_a + spread(send_a, n - 1 - t)
            out_b = out_b + spread(send_b, 1 + t)
            fin_a = got_a.astype(jnp.float32) + avg_l[(2 * n - 2 - t) % n].astype(jnp.float32)
            fin_b = got_b.astype(jnp.float32) + avg_r[(2 + t) % n].astype(jnp.float32)
            if t < n - 2:
                sum_a, sum_b = fin_a.astype(jnp.bfloat16), fin_b.astype(jnp.bfloat16)
        new_params = jnp.concatenate([out_a, out_b], axis=1)
        average_rows = jnp.concatenate([fin_a, fin_b], axis=1)
        return (
            new_params[None],
            new_master[None],
            new_first[None],
            new_second[None],
            average_rows[None],
        )

    return on_device


def solution(mesh):
    return jax.shard_map(
        make_on_device(ring_order(mesh)),
        mesh=mesh,
        in_specs=(
            P("dp", "mp", None, None),
            P(),
            P("mp", "dp", None),
            P("mp", "dp", None),
            P("mp", "dp", None),
            P("mp", "dp", None),
        ),
        out_specs=(
            P("mp", None, None),
            P("mp", "dp", None),
            P("mp", "dp", None),
            P("mp", "dp", None),
            P("mp", "dp", None),
        ),
        check_vma=False,
    )
```

```python
import math

import jax
import jax.numpy as jnp
from jax import lax
from jax.sharding import PartitionSpec as P


def ring_order(mesh):
    n = mesh.shape["dp"]
    try:
        coords = [tuple(mesh.devices[i, 0].coords) for i in range(n)]
        at = {(c[2], c[1]): i for i, c in enumerate(coords)}
        zs = sorted({z for z, _ in at})
        ys = sorted({y for _, y in at})
        if len(at) != n or len(zs) * len(ys) != n:
            return list(range(n))
        if len(ys) % 2:
            if len(zs) % 2:
                return list(range(n))
            at = {(y, z): i for (z, y), i in at.items()}
            zs, ys = ys, zs
        if len(zs) == 1 or len(ys) == 1:
            line = zs if len(ys) == 1 else ys
            return [at[(z, ys[0])] if len(ys) == 1 else at[(zs[0], z)] for z in line]
        cycle = [(z, ys[0]) for z in zs]
        for k, y in enumerate(ys[1:]):
            inner = zs[1:][::-1] if k % 2 == 0 else zs[1:]
            cycle += [(z, y) for z in inner]
        cycle += [(zs[0], y) for y in ys[1:][::-1]]
        return [at[c] for c in cycle]
    except (AttributeError, TypeError, IndexError, KeyError):
        return list(range(n))


def all_sum(v, axis, n):
    if n & (n - 1):
        return lax.psum(v, axis)
    k = 1
    while k < n:
        v = v + lax.ppermute(v, axis, [(i, i ^ k) for i in range(n)])
        k *= 2
    return v


def make_on_device(ring):
    n = len(ring)
    pos_of = [ring.index(r) for r in range(n)]
    fwd = [(ring[q], ring[(q + 1) % n]) for q in range(n)]
    bwd = [(ring[(q + 1) % n], ring[q]) for q in range(n)]

    def on_device(gradients, owner_list, master_weights, first_moment, second_moment, average_weights):
        local_grad = gradients[0, 0]
        nseg, seg = local_grad.shape
        cap = master_weights.shape[1]
        blocks = lax.axis_size("mp")
        per_rank = nseg // n
        half = seg // 2
        me = lax.axis_index("dp")
        mypos = jnp.array(pos_of, jnp.int32)[me]

        warm = jnp.zeros((8, 128), jnp.bfloat16)
        warm = lax.ppermute(warm, "dp", fwd) + lax.ppermute(warm, "dp", bwd)

        position = jnp.arange(nseg, dtype=jnp.int32)
        same_owner = (owner_list[:, None] == owner_list[None, :]) & (position[None, :] < position[:, None])
        within = jnp.sum(same_owner.astype(jnp.int32), axis=1)
        ahead = (jnp.array(pos_of, jnp.int32)[owner_list] - mypos + n) % n
        slot = ahead * cap + within
        hit = jnp.arange(n * cap, dtype=jnp.int32)[:, None] == slot[None, :]
        valid = jnp.any(hit[:cap], axis=1)
        placing = hit.astype(local_grad.dtype)
        left = jnp.dot(placing, local_grad[:, :half], preferred_element_type=jnp.bfloat16).reshape(n, cap, half)
        right = jnp.dot(placing, local_grad[:, half:], preferred_element_type=jnp.bfloat16).reshape(n, cap, half)

        send_a = left[n - 1] + warm[:1, :1]
        send_b = right[1]
        for t in range(n - 1):
            got_a = lax.ppermute(send_a, "dp", fwd)
            got_b = lax.ppermute(send_b, "dp", bwd)
            acc_a = got_a.astype(jnp.float32) + left[(2 * n - 2 - t) % n].astype(jnp.float32)
            acc_b = got_b.astype(jnp.float32) + right[(2 + t) % n].astype(jnp.float32)
            if t < n - 2:
                send_a, send_b = acc_a.astype(jnp.bfloat16), acc_b.astype(jnp.bfloat16)
        total_sq = all_sum(all_sum((jnp.sum(acc_a * acc_a) + jnp.sum(acc_b * acc_b)).reshape(1, 1), "dp", n), "mp", blocks)[0, 0]
        clip_factor = jnp.minimum(1.0, math.sqrt(blocks * nseg * seg) / (jnp.sqrt(total_sq) + 1e-06))
        in_use = valid.astype(jnp.float32)[:, None]

        def update(cols, grad):
            owned_grad = clip_factor * grad
            new_first = in_use * (0.9 * first_moment[0][:, cols] + 0.1 * owned_grad)
            new_second = in_use * (0.95 * second_moment[0][:, cols] + 0.05 * owned_grad * owned_grad)
            first_hat = new_first / (1.0 - 0.9**20)
            second_hat = new_second / (1.0 - 0.95**20)
            old_master = master_weights[0][:, cols]
            new_master = in_use * (
                old_master - 0.02 * (first_hat / (jnp.sqrt(second_hat) + 1e-08) + 0.1 * old_master)
            )
            averaged = 0.9 * average_weights[0][:, cols] + 0.1 * new_master
            return new_first, new_second, new_master, averaged

        upd_a = update(slice(0, half), acc_a)
        upd_b = update(slice(half, seg), acc_b)
        new_first, new_second, new_master = (jnp.concatenate([x, y], axis=1) for x, y in zip(upd_a[:3], upd_b[:3]))

        rank_ahead = jnp.array(ring, jnp.int32)[(mypos + jnp.arange(n, dtype=jnp.int32)) % n]
        seg_ahead = (rank_ahead[:, None] * per_rank + jnp.arange(per_rank, dtype=jnp.int32)[None, :]).reshape(-1)
        to_rows = (jnp.arange(cap, dtype=jnp.int32)[:, None] == slot[seg_ahead][None, :]).astype(jnp.bfloat16)
        avg_l, avg_r = (
            jnp.dot(to_rows.T, u[3].astype(jnp.bfloat16), preferred_element_type=jnp.bfloat16).reshape(n, per_rank, half)
            for u in (upd_a, upd_b)
        )
        send_a, send_b = upd_a[2].astype(jnp.bfloat16), upd_b[2].astype(jnp.bfloat16)
        placing_t = placing.T

        def spread(chunk, k):
            return jnp.dot(placing_t[:, k * cap:(k + 1) * cap], chunk, preferred_element_type=jnp.bfloat16)

        out_a = spread(send_a, 0)
        out_b = spread(send_b, 0)
        sum_a = avg_l[n - 1]
        sum_b = avg_r[1]
        for t in range(n - 1):
            send_a = lax.ppermute(send_a, "dp", fwd)
            send_b = lax.ppermute(send_b, "dp", bwd)
            got_a = lax.ppermute(sum_a, "dp", fwd)
            got_b = lax.ppermute(sum_b, "dp", bwd)
            if t == 0:
                new_master, new_first, new_second, send_a, send_b = lax.optimization_barrier(
                    (new_master, new_first, new_second, send_a, send_b)
                )
            out_a = out_a + spread(send_a, n - 1 - t)
            out_b = out_b + spread(send_b, 1 + t)
            fin_a = got_a.astype(jnp.float32) + avg_l[(2 * n - 2 - t) % n].astype(jnp.float32)
            fin_b = got_b.astype(jnp.float32) + avg_r[(2 + t) % n].astype(jnp.float32)
            if t < n - 2:
                sum_a, sum_b = fin_a.astype(jnp.bfloat16), fin_b.astype(jnp.bfloat16)
        new_params = jnp.concatenate([out_a, out_b], axis=1)
        average_rows = jnp.concatenate([fin_a, fin_b], axis=1)
        return (
            new_params[None],
            new_master[None],
            new_first[None],
            new_second[None],
            average_rows[None],
        )

    return on_device


def solution(mesh):
    return jax.shard_map(
        make_on_device(ring_order(mesh)),
        mesh=mesh,
        in_specs=(
            P("dp", "mp", None, None),
            P(),
            P("mp", "dp", None),
            P("mp", "dp", None),
            P("mp", "dp", None),
            P("mp", "dp", None),
        ),
        out_specs=(
            P("mp", None, None),
            P("mp", "dp", None),
            P("mp", "dp", None),
            P("mp", "dp", None),
            P("mp", "dp", None),
        ),
        check_vma=False,
    )
```

```python
import math

import jax
import jax.numpy as jnp
from jax import lax
from jax.sharding import PartitionSpec as P


def ring_order(mesh):
    n = mesh.shape["dp"]
    try:
        coords = [tuple(mesh.devices[i, 0].coords) for i in range(n)]
        at = {(c[2], c[1]): i for i, c in enumerate(coords)}
        zs = sorted({z for z, _ in at})
        ys = sorted({y for _, y in at})
        if len(at) != n or len(zs) * len(ys) != n:
            return list(range(n))
        if len(ys) % 2:
            if len(zs) % 2:
                return list(range(n))
            at = {(y, z): i for (z, y), i in at.items()}
            zs, ys = ys, zs
        if len(zs) == 1 or len(ys) == 1:
            line = zs if len(ys) == 1 else ys
            return [at[(z, ys[0])] if len(ys) == 1 else at[(zs[0], z)] for z in line]
        cycle = [(z, ys[0]) for z in zs]
        for k, y in enumerate(ys[1:]):
            inner = zs[1:][::-1] if k % 2 == 0 else zs[1:]
            cycle += [(z, y) for z in inner]
        cycle += [(zs[0], y) for y in ys[1:][::-1]]
        return [at[c] for c in cycle]
    except (AttributeError, TypeError, IndexError, KeyError):
        return list(range(n))


def all_sum(v, axis, n):
    if n & (n - 1):
        return lax.psum(v, axis)
    k = 1
    while k < n:
        v = v + lax.ppermute(v, axis, [(i, i ^ k) for i in range(n)])
        k *= 2
    return v


def make_on_device(ring):
    n = len(ring)
    pos_of = [ring.index(r) for r in range(n)]
    fwd = [(ring[q], ring[(q + 1) % n]) for q in range(n)]
    bwd = [(ring[(q + 1) % n], ring[q]) for q in range(n)]

    def on_device(gradients, owner_list, master_weights, first_moment, second_moment, average_weights):
        local_grad = gradients[0, 0]
        nseg, seg = local_grad.shape
        cap = master_weights.shape[1]
        blocks = lax.axis_size("mp")
        per_rank = nseg // n
        half = seg // 2
        me = lax.axis_index("dp")
        mypos = jnp.array(pos_of, jnp.int32)[me]

        warm = jnp.zeros((8, 128), jnp.bfloat16)
        warm = lax.ppermute(warm, "dp", fwd) + lax.ppermute(warm, "dp", bwd)

        position = jnp.arange(nseg, dtype=jnp.int32)
        same_owner = (owner_list[:, None] == owner_list[None, :]) & (position[None, :] < position[:, None])
        within = jnp.sum(same_owner.astype(jnp.int32), axis=1)
        ahead = (jnp.array(pos_of, jnp.int32)[owner_list] - mypos + n) % n
        slot = ahead * cap + within
        hit = jnp.arange(n * cap, dtype=jnp.int32)[:, None] == slot[None, :]
        valid = jnp.any(hit[:cap], axis=1)
        placing = hit.astype(local_grad.dtype)
        left = jnp.dot(placing, local_grad[:, :half], preferred_element_type=jnp.bfloat16).reshape(n, cap, half)
        right = jnp.dot(placing, local_grad[:, half:], preferred_element_type=jnp.bfloat16).reshape(n, cap, half)

        send_a = left[n - 1] + warm[:1, :1]
        send_b = right[1]
        for t in range(n - 1):
            got_a = lax.ppermute(send_a, "dp", fwd)
            got_b = lax.ppermute(send_b, "dp", bwd)
            acc_a = got_a.astype(jnp.float32) + left[(2 * n - 2 - t) % n].astype(jnp.float32)
            acc_b = got_b.astype(jnp.float32) + right[(2 + t) % n].astype(jnp.float32)
            if t < n - 2:
                send_a, send_b = acc_a.astype(jnp.bfloat16), acc_b.astype(jnp.bfloat16)
        total_sq = all_sum(all_sum((jnp.sum(acc_a * acc_a) + jnp.sum(acc_b * acc_b)).reshape(1, 1), "mp", blocks), "dp", n)[0, 0]
        clip_factor = jnp.minimum(1.0, math.sqrt(blocks * nseg * seg) / (jnp.sqrt(total_sq) + 1e-06))
        in_use = valid.astype(jnp.float32)[:, None]

        def update(cols, grad):
            owned_grad = clip_factor * grad
            new_first = in_use * (0.9 * first_moment[0][:, cols] + 0.1 * owned_grad)
            new_second = in_use * (0.95 * second_moment[0][:, cols] + 0.05 * owned_grad * owned_grad)
            first_hat = new_first / (1.0 - 0.9**20)
            second_hat = new_second / (1.0 - 0.95**20)
            old_master = master_weights[0][:, cols]
            new_master = in_use * (
                old_master - 0.02 * (first_hat / (jnp.sqrt(second_hat) + 1e-08) + 0.1 * old_master)
            )
            averaged = 0.9 * average_weights[0][:, cols] + 0.1 * new_master
            return new_first, new_second, new_master, averaged

        upd_a = update(slice(0, half), acc_a)
        upd_b = update(slice(half, seg), acc_b)
        new_first, new_second, new_master = (jnp.concatenate([x, y], axis=1) for x, y in zip(upd_a[:3], upd_b[:3]))

        rank_ahead = jnp.array(ring, jnp.int32)[(mypos + jnp.arange(n, dtype=jnp.int32)) % n]
        seg_ahead = (rank_ahead[:, None] * per_rank + jnp.arange(per_rank, dtype=jnp.int32)[None, :]).reshape(-1)
        to_rows = (jnp.arange(cap, dtype=jnp.int32)[:, None] == slot[seg_ahead][None, :]).astype(jnp.bfloat16)
        avg_l, avg_r = (
            jnp.dot(to_rows.T, u[3].astype(jnp.bfloat16), preferred_element_type=jnp.bfloat16).reshape(n, per_rank, half)
            for u in (upd_a, upd_b)
        )
        send_a, send_b = upd_a[2].astype(jnp.bfloat16), upd_b[2].astype(jnp.bfloat16)
        placing_t = placing.T

        def spread(chunk, k):
            return jnp.dot(placing_t[:, k * cap:(k + 1) * cap], chunk, preferred_element_type=jnp.bfloat16)

        out_a = spread(send_a, 0)
        out_b = spread(send_b, 0)
        sum_a = avg_l[n - 1]
        sum_b = avg_r[1]
        for t in range(n - 1):
            send_a = lax.ppermute(send_a, "dp", fwd)
            send_b = lax.ppermute(send_b, "dp", bwd)
            got_a = lax.ppermute(sum_a, "dp", fwd)
            got_b = lax.ppermute(sum_b, "dp", bwd)
            if t == 0:
                new_master, new_first, new_second, send_a, send_b = lax.optimization_barrier(
                    (new_master, new_first, new_second, send_a, send_b)
                )
            out_a = out_a + spread(send_a, n - 1 - t)
            out_b = out_b + spread(send_b, 1 + t)
            fin_a = got_a.astype(jnp.float32) + avg_l[(2 * n - 2 - t) % n].astype(jnp.float32)
            fin_b = got_b.astype(jnp.float32) + avg_r[(2 + t) % n].astype(jnp.float32)
            if t < n - 2:
                sum_a, sum_b = fin_a.astype(jnp.bfloat16), fin_b.astype(jnp.bfloat16)
        new_params = jnp.concatenate([out_a, out_b], axis=1)
        average_rows = jnp.concatenate([fin_a, fin_b], axis=1)
        return (
            new_params[None],
            new_master[None],
            new_first[None],
            new_second[None],
            average_rows[None],
        )

    return on_device


def solution(mesh):
    return jax.shard_map(
        make_on_device(ring_order(mesh)),
        mesh=mesh,
        in_specs=(
            P("dp", "mp", None, None),
            P(),
            P("mp", "dp", None),
            P("mp", "dp", None),
            P("mp", "dp", None),
            P("mp", "dp", None),
        ),
        out_specs=(
            P("mp", None, None),
            P("mp", "dp", None),
            P("mp", "dp", None),
            P("mp", "dp", None),
            P("mp", "dp", None),
        ),
        check_vma=False,
    )
```
